128 devices in a mesh: grp: 8 (over x, core), seq: 16 (over z, y).
Axes of the slice: x: 4, y: 4, z: 4, core: 2. Of those that a mesh axis runs over, the one named last changes fastest.
Arguments:
- queries: bfloat16 [16384, 4096], P(('grp', 'seq')), may hold values from -6 to 6
- kv_pairs: bfloat16 [2, 16384, 256], P(None, ('grp', 'seq')), may hold values from -6 to 6
- residual: bfloat16 [16384, 4096], P(('grp', 'seq')), may hold values from -30 to 30
- norm_gain: bfloat16 [4096], replicated, may hold values from 0.099609375 to 1.8984375
- o_weight: bfloat16 [4096, 4096], P('seq'), may hold values from -0.09375 to 0.09375
- w_in: bfloat16 [128, 4096, 1536], P(('grp', 'seq')), may hold values from -0.09375 to 0.09375
- w_down: bfloat16 [128, 768, 4096], P(('grp', 'seq')), may hold values from -0.21875 to 0.21875
- expert_ids: int32 [16384, 4], P(('grp', 'seq')), may hold values from 0 to 127, all different within a row; in each aligned block of 128 rows (0 to 127, 128 to 255, ...) at most 8 rows name the same one
- route_weights: float32 [16384, 4], P(('grp', 'seq')), may hold values from 0.1 to 0.6
Outputs:
- layer_out: bfloat16 [16384, 4096], P(('grp', 'seq'))
The draws below stay inside these ranges and needn't reach their ends.
Inputs may be any that keep to these rules, and one draw needn't show every extreme that they name: `expert_ids`: within the rows of one device (aligned blocks of 128 rows) no expert is named by more than 8 rows, a bound that some block reaches; each row names 4 different experts, and every expert is named somewhere.
All inputs are finite; a program needn't handle non-finite values.
Results may differ from the reference program's by a relative error of at most 0.01.
Values may be sent and summed in bfloat16 or wider, within the bound.
No kernel may reach another device: no remote copies, remote signals or barrier semaphores. Data moves between devices by JAX's collectives and lax.ppermute only.
A program may use at most 128 MiB of HBM per device.

```python
import math
import jax
import jax.numpy as jnp
import numpy as np
from jax import lax

D = 4096
HEADS = 32
KVH = 2
HD = 128
FFE = 768
TOPK = 4
TOK_DEV = 128
EXPERTS = 128
CAP = 8
SEQ_LEN = 2048
TOKENS = 16384
HPD = 2
GROUP = 16
N_GRP = 8
N_SEQ = 16


def draw_queries(key, part):
    base = jnp.clip(jax.random.normal(jax.random.fold_in(key, 11), (TOKENS, HEADS, HD), jnp.float32), -5.5, 5.5)
    return base.reshape(TOKENS, HEADS * HD).astype(jnp.bfloat16)


def draw_kv_pairs(key, part):
    keys_part = jnp.clip(jax.random.normal(jax.random.fold_in(key, 21), (TOKENS, KVH, HD), jnp.float32), -5.5, 5.5)
    values_part = jnp.clip(jax.random.normal(jax.random.fold_in(key, 22), (TOKENS, KVH, HD), jnp.float32), -5.5, 5.5)
    stacked = jnp.stack([keys_part, values_part])
    return stacked.reshape(2, TOKENS, KVH * HD).astype(jnp.bfloat16)


def draw_residual(key, part):
    row_scale = jnp.exp(jax.random.uniform(jax.random.fold_in(key, 31), (TOKENS, 1), jnp.float32, math.log(0.3), math.log(3.0)))
    col_scale = jnp.exp(jax.random.uniform(jax.random.fold_in(key, 32), (1, D), jnp.float32, math.log(0.5), math.log(2.0)))
    base = jnp.clip(jax.random.normal(jax.random.fold_in(key, 33), (TOKENS, D), jnp.float32), -4.0, 4.0)
    return (base * row_scale * col_scale).astype(jnp.bfloat16)


def shard_levels(rng, extent, shards, least, high):
    level, own = 1.0, jax.random.fold_in(rng, 6)
    for axis_at, parts in shards:
        heights = jnp.exp(jax.random.uniform(jax.random.fold_in(own, axis_at), (parts,), jnp.float32, least / len(shards), high / len(shards)))
        level = level * jnp.repeat(heights, extent[axis_at] // parts).reshape([-1 if axis == axis_at else 1 for axis in range(len(extent))])
    return level


def shared_out(rng, own, number, rows, number_of, top, most, lean):
    sequence = jax.random.permutation(rng, number_of)
    heavy_load, usual = load_shares(number_of, rows * top, most, lean, True), load_shares(number_of, rows * top, most, lean, False)
    places = jnp.arange(number_of)

    def named(tallies, turn):
        used = int((tallies > 0).sum())
        fixed = max(1, used // 4)
        passed = fixed + (places - fixed + turn * (used - fixed)) % max(1, number_of - fixed)
        return jnp.zeros((number_of,), jnp.int32).at[sequence[jnp.where(places < fixed, places, passed)]].set(jnp.asarray(tallies, jnp.int32))

    tallies = jnp.where(number % 4 == 0, named(heavy_load, number // 4), named(usual, number - number // 4 - 1))
    mixed = jax.random.permutation(jax.random.fold_in(own, 3), number_of)
    source_of, receiver = mixed[0:number_of // 2 * 2:2], mixed[1:number_of // 2 * 2:2]
    room = jnp.minimum(tallies[source_of] - 1, most - tallies[receiver]) // 2
    room = jnp.where((source_of == sequence[0]) | (receiver == sequence[0]) | (tallies[receiver] == 0), 0, jnp.maximum(room, 0))
    passed = jax.random.randint(jax.random.fold_in(own, 4), (number_of // 2,), 0, 1 << 20) % (room + 1)
    tallies = tallies.at[source_of].add(-passed).at[receiver].add(passed)
    members = jnp.searchsorted(jnp.cumsum(tallies), jnp.arange(rows * top), side="right").astype(jnp.int32)
    table = members.reshape(top, rows).T
    table = table[jax.random.permutation(jax.random.fold_in(own, 1), rows)]
    turn = jax.random.randint(jax.random.fold_in(own, 2), (rows, 1), 0, top)
    return jnp.take_along_axis(table, (jnp.arange(top)[None, :] + turn) % top, axis=1)


def load_shares(count, total, bound, slope, full):
    weights = [(1 << 20) // math.isqrt(rank ** slope) + 1 for rank in range(1, count + 1)]
    largest = bound if full else min(bound, max(-(-total // count), total * weights[0] // sum(weights)))
    least = 1 if total - largest >= count - 1 else 0
    holding, spare = [largest] + [least] * (count - 1), total - largest - least * (count - 1)
    while spare > 0:
        candidates = [i for i in range(1, count) if holding[i] < largest] or [i for i in range(1, count) if holding[i] < bound]
        pool, budget = sum([weights[i] for i in candidates]), spare
        for i in candidates:
            more = min(bound - holding[i], max(1, budget * weights[i] // pool), spare)
            holding[i] = holding[i] + more
            spare = spare - more
    return np.array(holding)


def scatter_about(own_key, dims, deviation, reach, cuts=(), held_as=jnp.bfloat16):
    values = jax.random.normal(own_key, dims, jnp.float32) * deviation
    if len(cuts) > 0:
        values = shard_levels(own_key, dims, cuts, -0.22, 0.18) * values
    return jnp.clip(values, min=-reach, max=reach).astype(held_as)


def setup_inputs(seed: int = 0) -> dict:
    seeds = jax.random.split(jax.random.key(seed), 10)
    queries = draw_queries(jax.random.fold_in(seeds[9], 71), 0)
    kv_pairs = draw_kv_pairs(jax.random.fold_in(seeds[9], 71), 0)
    residual = draw_residual(jax.random.fold_in(seeds[9], 71), 0)
    norm_gain = jnp.clip(1.0 + 0.18 * jax.random.normal(seeds[3], (D,), jnp.float32), 0.099609375, 1.8984375).astype(jnp.bfloat16)
    o_weight = scatter_about(seeds[4], (HEADS * HD, D), (HEADS * HD) ** -0.5, 0.09375, ((0, 16),))
    w_in = scatter_about(seeds[5], (EXPERTS, D, 2 * FFE), D ** -0.5, 0.09375, ((0, 128),))
    w_down = scatter_about(seeds[6], (EXPERTS, FFE, D), FFE ** -0.5, 0.21875, ((0, 128),))
    expert_ids_keys = jax.random.split(jax.random.fold_in(seeds[7], 1), TOKENS // TOK_DEV)
    expert_ids_turns = jax.random.permutation(jax.random.fold_in(seeds[7], 3), TOKENS // TOK_DEV)
    expert_ids = jax.vmap(lambda own, number: shared_out(jax.random.fold_in(seeds[7], 2), own, number, TOK_DEV, EXPERTS, TOPK, CAP, 2))(expert_ids_keys, expert_ids_turns).reshape((TOKENS, TOPK))
    route_weights = jnp.clip(0.1 + 0.5 * jax.random.uniform(seeds[8], (TOKENS, TOPK), jnp.float32) ** shard_levels(seeds[8], (TOKENS, TOPK), ((0, 128),), -0.2, 0.2), 0.1, 0.6)
    return {"queries": queries, "kv_pairs": kv_pairs, "residual": residual, "norm_gain": norm_gain, "o_weight": o_weight, "w_in": w_in, "w_down": w_down, "expert_ids": expert_ids, "route_weights": route_weights}


def head_attention(operands):
    query_rows, key_rows, value_rows = operands
    length = query_rows.shape[0]
    scores = jnp.dot(query_rows, key_rows.T, preferred_element_type=jnp.float32) * (1.0 / HD ** 0.5)
    positions = jnp.arange(length, dtype=jnp.int32)
    allowed = positions[None, :] <= positions[:, None]
    scores = jnp.where(allowed, scores, jnp.float32(-1e+30))
    top_score = lax.optimization_barrier(jnp.max(scores, axis=1, keepdims=True))
    weights = jnp.exp(scores - top_score)
    probs = (weights / lax.optimization_barrier(jnp.sum(weights, axis=1, keepdims=True))).astype(jnp.bfloat16)
    return jnp.dot(probs, value_rows, preferred_element_type=jnp.float32).astype(jnp.bfloat16)

def sequence_attention(operands):
    query_seq, key_seq, value_seq, o_blocks = operands
    query_heads = query_seq.reshape(SEQ_LEN, HEADS, HD).transpose(1, 0, 2)
    key_heads = jnp.repeat(key_seq.reshape(SEQ_LEN, KVH, HD).transpose(1, 0, 2), GROUP, axis=0)
    value_heads = jnp.repeat(value_seq.reshape(SEQ_LEN, KVH, HD).transpose(1, 0, 2), GROUP, axis=0)
    attended = lax.map(head_attention, (query_heads, key_heads, value_heads))
    blocks = attended.reshape(N_SEQ, HPD, SEQ_LEN, HD).transpose(0, 2, 1, 3).reshape(N_SEQ, SEQ_LEN, HPD * HD)

    def add_block(total, pair):
        block_rows, block_weight = pair
        partial_j = jnp.dot(block_rows, block_weight, preferred_element_type=jnp.float32).astype(jnp.bfloat16)
        return (total + partial_j.astype(jnp.float32), None)
    total, unused = lax.scan(add_block, jnp.zeros((SEQ_LEN, D), jnp.float32), (blocks, o_blocks))
    return total

def reference(queries, kv_pairs, residual, norm_gain, o_weight, w_in, w_down, expert_ids, route_weights):
    query_seqs = queries.reshape(N_GRP, SEQ_LEN, HEADS * HD)
    key_seqs = kv_pairs[0].reshape(N_GRP, SEQ_LEN, KVH * HD)
    value_seqs = kv_pairs[1].reshape(N_GRP, SEQ_LEN, KVH * HD)
    o_blocks = o_weight.reshape(N_SEQ, HPD * HD, D)
    attn_out = lax.map(lambda trio: sequence_attention((trio[0], trio[1], trio[2], o_blocks)), (query_seqs, key_seqs, value_seqs))
    attn_out = attn_out.reshape(TOKENS, D)
    mixed = residual.astype(jnp.float32) + attn_out
    mean_square = lax.optimization_barrier(jnp.mean(mixed * mixed, axis=1, keepdims=True))
    normed = (mixed * lax.rsqrt(mean_square + 1e-06) * norm_gain.astype(jnp.float32)).astype(jnp.bfloat16)
    flat_ids = expert_ids.reshape(-1)
    flat_weights = route_weights.reshape(-1)
    slots_total = EXPERTS * CAP

    def one_expert(total, operands):
        expert_index, gate_up, down = operands
        chosen = flat_ids == expert_index
        places = jnp.nonzero(chosen, size=slots_total, fill_value=0)[0].astype(jnp.int32)
        count = jnp.sum(chosen.astype(jnp.int32))
        valid = jnp.arange(slots_total, dtype=jnp.int32) < count
        token_rows = (places // TOPK).astype(jnp.int32)
        inputs = normed[token_rows]
        projected = jnp.dot(inputs, gate_up, preferred_element_type=jnp.float32)
        hidden = (jax.nn.silu(projected[:, :FFE]) * projected[:, FFE:]).astype(jnp.bfloat16)
        expert_out = jnp.dot(hidden, down, preferred_element_type=jnp.float32).astype(jnp.bfloat16)
        scaled = expert_out.astype(jnp.float32) * jnp.where(valid, flat_weights[places], jnp.float32(0.0))[:, None]
        return (total.at[token_rows].add(scaled), None)
    combined, unused = lax.scan(one_expert, jnp.zeros((TOKENS, D), jnp.float32), (jnp.arange(EXPERTS, dtype=jnp.int32), w_in, w_down))
    return (mixed + combined).astype(jnp.bfloat16)
```

```python
import functools

import jax
import jax.numpy as jnp
from jax import lax
from jax.experimental import pallas as pl
from jax.experimental.pallas import tpu as pltpu
from jax.sharding import PartitionSpec as P

HD = 128
Q_BLOCK = 256


def _attend_kernel(q_ref, k_ref, v_ref, o_ref, *, block, scale):
    qi = pl.program_id(1)
    q = q_ref[...]
    k = k_ref[...]
    length = k.shape[0]
    scores = lax.dot_general(
        q, k, (((1,), (1,)), ((), ())), preferred_element_type=jnp.float32
    ) * scale
    q_pos = qi * block + lax.broadcasted_iota(jnp.int32, (block, length), 0)
    k_pos = lax.broadcasted_iota(jnp.int32, (block, length), 1)
    scores = jnp.where(k_pos <= q_pos, scores, jnp.float32(-1e30))
    top = jnp.max(scores, axis=1, keepdims=True)
    weights = jnp.exp(scores - top)
    total = jnp.sum(weights, axis=1, keepdims=True)
    probs = (weights / total).astype(jnp.bfloat16)
    o_ref[...] = jnp.dot(probs, v_ref[...], preferred_element_type=jnp.float32).astype(
        o_ref.dtype
    )


def attention(packed, heads, head_size):
    seq_len = packed.shape[0]
    block = min(Q_BLOCK, seq_len)
    kernel = functools.partial(_attend_kernel, block=block, scale=1.0 / head_size**0.5)
    return pl.pallas_call(
        kernel,
        out_shape=jax.ShapeDtypeStruct((seq_len, heads * head_size), jnp.bfloat16),
        grid=(heads, seq_len // block),
        in_specs=[
            pl.BlockSpec((block, head_size), lambda h, i: (i, h)),
            pl.BlockSpec((seq_len, head_size), lambda h, i: (0, heads)),
            pl.BlockSpec((seq_len, head_size), lambda h, i: (0, heads + 1)),
        ],
        out_specs=pl.BlockSpec((block, head_size), lambda h, i: (i, h)),
        compiler_params=pltpu.CompilerParams(
            dimension_semantics=("arbitrary", "arbitrary"),
            vmem_limit_bytes=48 * 1024 * 1024,
        ),
    )(packed, packed, packed)


def shards(
    queries, kv_pairs, residual, norm_gain, o_weight, w_in, w_down, expert_ids, route_weights
):
    tok_dev = queries.shape[0]
    width = residual.shape[1]
    n_seq = lax.axis_size("seq")
    n_grp = lax.axis_size("grp")
    devices = n_seq * n_grp
    head_size = HD
    heads_all = queries.shape[1] // head_size
    per_device = heads_all // n_seq
    key_heads = kv_pairs.shape[2] // head_size
    sharing = heads_all // key_heads
    assert sharing % per_device == 0

    q_send = queries.reshape(tok_dev, n_seq, per_device * head_size).transpose(1, 0, 2)
    kv_heads = kv_pairs.reshape(2, tok_dev, key_heads, head_size)
    head_of_dest = (jnp.arange(n_seq) * per_device) // sharing
    kv_send = jnp.take(kv_heads, head_of_dest, axis=2)
    kv_send = kv_send.transpose(2, 1, 0, 3).reshape(n_seq, tok_dev, 2 * head_size)
    send = jnp.concatenate([q_send, kv_send], axis=2)
    packed = lax.all_to_all(send, "seq", split_axis=0, concat_axis=0, tiled=True)
    seq_len = n_seq * tok_dev
    packed = packed.reshape(seq_len, (per_device + 2) * head_size)

    attended = attention(packed, per_device, head_size)
    attn_out = lax.psum_scatter(
        jnp.dot(attended, o_weight, preferred_element_type=jnp.float32).astype(jnp.bfloat16),
        "seq",
        scatter_dimension=0,
        tiled=True,
    ).astype(jnp.float32)
    mixed = residual.astype(jnp.float32) + attn_out
    mean_square = jnp.mean(mixed * mixed, axis=1, keepdims=True)
    normed = (mixed * lax.rsqrt(mean_square + 1e-06) * norm_gain.astype(jnp.float32)).astype(
        jnp.bfloat16
    )

    top_count = expert_ids.shape[1]
    capacity = 2 * tok_dev * top_count // devices
    slots = devices * capacity
    flat_ids = expert_ids.reshape(-1)
    flat_weights = route_weights.reshape(-1)
    n_flat = flat_ids.shape[0]
    onehot = (flat_ids[:, None] == jnp.arange(devices, dtype=jnp.int32)[None, :]).astype(
        jnp.bfloat16
    )
    row = lax.broadcasted_iota(jnp.int32, (n_flat, n_flat), 0)
    col = lax.broadcasted_iota(jnp.int32, (n_flat, n_flat), 1)
    before = (col < row).astype(jnp.bfloat16)
    earlier = jnp.dot(before, onehot, preferred_element_type=jnp.float32)
    rank = jnp.sum(earlier * onehot.astype(jnp.float32), axis=1).astype(jnp.int32)
    slot_index = flat_ids * capacity + rank
    picks = slot_index[:, None] == jnp.arange(slots, dtype=jnp.int32)[None, :]
    token_slots = jnp.any(picks.reshape(tok_dev, top_count, slots), axis=1).astype(jnp.bfloat16)
    outgoing_rows = lax.dot_general(
        token_slots, normed, (((0,), (0,)), ((), ())), preferred_element_type=jnp.float32
    ).astype(jnp.bfloat16)
    outgoing_rows = outgoing_rows.reshape(devices, capacity, width)
    ffe_width = w_down.shape[1]
    arrived = lax.all_to_all(outgoing_rows, ("grp", "seq"), split_axis=0, concat_axis=0, tiled=True)
    flat_rows = arrived.reshape(-1, width)
    projected = jnp.dot(flat_rows, w_in[0], preferred_element_type=jnp.float32)
    hidden = (jax.nn.silu(projected[:, :ffe_width]) * projected[:, ffe_width:]).astype(jnp.bfloat16)
    produced = jnp.dot(hidden, w_down[0], preferred_element_type=jnp.float32).astype(jnp.bfloat16)
    returned = lax.all_to_all(
        produced.reshape(arrived.shape), ("grp", "seq"), split_axis=0, concat_axis=0, tiled=True
    )
    returned = returned.reshape(slots, width)
    picked = jnp.dot(picks.astype(jnp.bfloat16), returned, preferred_element_type=jnp.float32)
    picked = picked * flat_weights[:, None]
    combined = jnp.sum(picked.reshape(tok_dev, top_count, width), axis=1)
    return (mixed + combined).astype(jnp.bfloat16)


def solution(mesh):
    return jax.shard_map(
        shards,
        mesh=mesh,
        in_specs=(
            P(("grp", "seq"), None),
            P(None, ("grp", "seq"), None),
            P(("grp", "seq"), None),
            P(),
            P("seq", None),
            P(("grp", "seq"), None, None),
            P(("grp", "seq"), None, None),
            P(("grp", "seq"), None),
            P(("grp", "seq"), None),
        ),
        out_specs=P(("grp", "seq"), None),
        check_vma=False,
    )
```

```python
import functools

import jax
import jax.numpy as jnp
from jax import lax
from jax.experimental import pallas as pl
from jax.experimental.pallas import tpu as pltpu
from jax.sharding import PartitionSpec as P

HD = 128
Q_BLOCK = 256


def _attend_kernel(q_ref, k_ref, v_ref, o_ref, *, block, scale):
    qi = pl.program_id(1)
    q = q_ref[...]
    k = k_ref[...]
    length = k.shape[0]
    scores = lax.dot_general(
        q, k, (((1,), (1,)), ((), ())), preferred_element_type=jnp.float32
    ) * scale
    q_pos = qi * block + lax.broadcasted_iota(jnp.int32, (block, length), 0)
    k_pos = lax.broadcasted_iota(jnp.int32, (block, length), 1)
    scores = jnp.where(k_pos <= q_pos, scores, jnp.float32(-1e30))
    top = jnp.max(scores, axis=1, keepdims=True)
    weights = jnp.exp(scores - top)
    total = jnp.sum(weights, axis=1, keepdims=True)
    probs = (weights / total).astype(jnp.bfloat16)
    o_ref[...] = jnp.dot(probs, v_ref[...], preferred_element_type=jnp.float32).astype(
        o_ref.dtype
    )


def attention(packed, heads, head_size):
    seq_len = packed.shape[0]
    block = min(Q_BLOCK, seq_len)
    kernel = functools.partial(_attend_kernel, block=block, scale=1.0 / head_size**0.5)
    return pl.pallas_call(
        kernel,
        out_shape=jax.ShapeDtypeStruct((seq_len, heads * head_size), jnp.bfloat16),
        grid=(heads, seq_len // block),
        in_specs=[
            pl.BlockSpec((block, head_size), lambda h, i: (i, h)),
            pl.BlockSpec((seq_len, head_size), lambda h, i: (0, heads)),
            pl.BlockSpec((seq_len, head_size), lambda h, i: (0, heads + 1)),
        ],
        out_specs=pl.BlockSpec((block, head_size), lambda h, i: (i, h)),
        compiler_params=pltpu.CompilerParams(
            dimension_semantics=("arbitrary", "arbitrary"),
            vmem_limit_bytes=48 * 1024 * 1024,
        ),
    )(packed, packed, packed)


def shards(
    queries, kv_pairs, residual, norm_gain, o_weight, w_in, w_down, expert_ids, route_weights
):
    tok_dev = queries.shape[0]
    width = residual.shape[1]
    n_seq = lax.axis_size("seq")
    n_grp = lax.axis_size("grp")
    devices = n_seq * n_grp
    head_size = HD
    heads_all = queries.shape[1] // head_size
    per_device = heads_all // n_seq
    key_heads = kv_pairs.shape[2] // head_size
    sharing = heads_all // key_heads
    assert sharing % per_device == 0

    q_send = queries.reshape(tok_dev, n_seq, per_device * head_size).transpose(1, 0, 2)
    kv_heads = kv_pairs.reshape(2, tok_dev, key_heads, head_size)
    head_of_dest = (jnp.arange(n_seq) * per_device) // sharing
    kv_send = jnp.take(kv_heads, head_of_dest, axis=2)
    kv_send = kv_send.transpose(2, 1, 0, 3).reshape(n_seq, tok_dev, 2 * head_size)
    send = jnp.concatenate([q_send, kv_send], axis=2)
    packed = lax.all_to_all(send, "seq", split_axis=0, concat_axis=0, tiled=True)
    seq_len = n_seq * tok_dev
    packed = packed.reshape(seq_len, (per_device + 2) * head_size)

    attended = attention(packed, per_device, head_size)
    attn_out = lax.psum_scatter(
        jnp.dot(attended, o_weight, preferred_element_type=jnp.float32).astype(jnp.bfloat16),
        "seq",
        scatter_dimension=0,
        tiled=True,
    ).astype(jnp.float32)
    mixed = residual.astype(jnp.float32) + attn_out
    mean_square = jnp.mean(mixed * mixed, axis=1, keepdims=True)
    normed = (mixed * lax.rsqrt(mean_square + 1e-06) * norm_gain.astype(jnp.float32)).astype(
        jnp.bfloat16
    )

    top_count = expert_ids.shape[1]
    capacity = 2 * tok_dev * top_count // devices
    slots = devices * capacity
    flat_ids = expert_ids.reshape(-1)
    flat_weights = route_weights.reshape(-1)
    n_flat = flat_ids.shape[0]
    onehot = (flat_ids[:, None] == jnp.arange(devices, dtype=jnp.int32)[None, :]).astype(
        jnp.bfloat16
    )
    row = lax.broadcasted_iota(jnp.int32, (n_flat, n_flat), 0)
    col = lax.broadcasted_iota(jnp.int32, (n_flat, n_flat), 1)
    before = (col < row).astype(jnp.bfloat16)
    earlier = jnp.dot(before, onehot, preferred_element_type=jnp.float32)
    rank = jnp.sum(earlier * onehot.astype(jnp.float32), axis=1).astype(jnp.int32)
    slot_index = flat_ids * capacity + rank
    picks = slot_index[:, None] == jnp.arange(slots, dtype=jnp.int32)[None, :]
    token_slots = jnp.any(picks.reshape(tok_dev, top_count, slots), axis=1).astype(jnp.bfloat16)
    outgoing_rows = lax.dot_general(
        token_slots, normed, (((0,), (0,)), ((), ())), preferred_element_type=jnp.float32
    ).astype(jnp.bfloat16)
    outgoing_rows = outgoing_rows.reshape(devices, capacity, width)
    ffe_width = w_down.shape[1]
    arrived = lax.all_to_all(outgoing_rows, ("grp", "seq"), split_axis=0, concat_axis=0, tiled=True)
    flat_rows = arrived.reshape(-1, width)
    projected = jnp.dot(flat_rows, w_in[0], preferred_element_type=jnp.float32)
    hidden = (jax.nn.silu(projected[:, :ffe_width]) * projected[:, ffe_width:]).astype(jnp.bfloat16)
    produced = jnp.dot(hidden, w_down[0], preferred_element_type=jnp.float32).astype(jnp.bfloat16)
    returned = lax.all_to_all(
        produced.reshape(arrived.shape), ("grp", "seq"), split_axis=0, concat_axis=0, tiled=True
    )
    returned = returned.reshape(slots, width)
    picks_by_choice = picks.reshape(tok_dev, top_count, slots).transpose(1, 0, 2)
    picked = jnp.dot(
        picks_by_choice.reshape(n_flat, slots).astype(jnp.bfloat16),
        returned,
        preferred_element_type=jnp.float32,
    ).reshape(top_count, tok_dev, width)
    weights_by_choice = route_weights.T.reshape(top_count, tok_dev, 1)
    combined = jnp.sum(picked * weights_by_choice, axis=0)
    return (mixed + combined).astype(jnp.bfloat16)


def solution(mesh):
    return jax.shard_map(
        shards,
        mesh=mesh,
        in_specs=(
            P(("grp", "seq"), None),
            P(None, ("grp", "seq"), None),
            P(("grp", "seq"), None),
            P(),
            P("seq", None),
            P(("grp", "seq"), None, None),
            P(("grp", "seq"), None, None),
            P(("grp", "seq"), None),
            P(("grp", "seq"), None),
        ),
        out_specs=P(("grp", "seq"), None),
        check_vma=False,
    )
```

```python
import functools
import math

import jax
import jax.numpy as jnp
from jax import lax
from jax.experimental import pallas as pl
from jax.experimental.pallas import tpu as pltpu
from jax.sharding import Mesh, PartitionSpec as P

HD = 128
Q_BLOCK = 256


def _attend_kernel(meta_ref, q_ref, k_ref, v_ref, o_ref, *, block, scale, tok_dev, n_sb):
    qi = pl.program_id(1)
    sb = meta_ref[0]
    q = q_ref[...]
    k = k_ref[...]
    length = k.shape[0]
    scores = lax.dot_general(
        q, k, (((1,), (1,)), ((), ())), preferred_element_type=jnp.float32
    ) * scale
    local = qi * block + lax.broadcasted_iota(jnp.int32, (block, length), 0)
    q_pos = ((local // tok_dev) * n_sb + sb) * tok_dev + local % tok_dev
    k_pos = lax.broadcasted_iota(jnp.int32, (block, length), 1)
    scores = jnp.where(k_pos <= q_pos, scores, jnp.float32(-1e30))
    top = jnp.max(scores, axis=1, keepdims=True)
    weights = jnp.exp(scores - top)
    total = jnp.sum(weights, axis=1, keepdims=True)
    probs = (weights / total).astype(jnp.bfloat16)
    o_ref[...] = jnp.dot(probs, v_ref[...], preferred_element_type=jnp.float32).astype(
        o_ref.dtype
    )


def attention(meta, q_rows, kv_all, heads, head_size, tok_dev, n_sb):
    rows = q_rows.shape[0]
    seq_len = kv_all.shape[1]
    block = min(Q_BLOCK, rows)
    kernel = functools.partial(
        _attend_kernel, block=block, scale=1.0 / head_size**0.5, tok_dev=tok_dev, n_sb=n_sb
    )
    return pl.pallas_call(
        kernel,
        out_shape=jax.ShapeDtypeStruct((rows, heads * head_size), jnp.bfloat16),
        grid_spec=pltpu.PrefetchScalarGridSpec(
            num_scalar_prefetch=1,
            grid=(heads, rows // block),
            in_specs=[
                pl.BlockSpec((block, head_size), lambda h, i, m: (i, h)),
                pl.BlockSpec((None, seq_len, head_size), lambda h, i, m: (0, 0, m[1])),
                pl.BlockSpec((None, seq_len, head_size), lambda h, i, m: (1, 0, m[1])),
            ],
            out_specs=pl.BlockSpec((block, head_size), lambda h, i, m: (i, h)),
        ),
        compiler_params=pltpu.CompilerParams(
            dimension_semantics=("arbitrary", "arbitrary"),
            vmem_limit_bytes=48 * 1024 * 1024,
        ),
    )(meta, q_rows, kv_all, kv_all)


def shards(
    queries, kv_pairs, residual, norm_gain, o_weight, w_in, w_down, expert_ids, route_weights
):
    tok_dev = queries.shape[0]
    width = residual.shape[1]
    n_sa = lax.axis_size("sa")
    n_sb = lax.axis_size("sb")
    n_seq = n_sa * n_sb
    n_grp = lax.axis_size("grp")
    devices = n_seq * n_grp
    head_size = HD
    heads_all = queries.shape[1] // head_size
    key_heads = kv_pairs.shape[2] // head_size
    sharing = heads_all // key_heads
    heads_here = heads_all // n_sa
    block_rows = o_weight.shape[0]
    assert sharing % heads_here == 0
    sa = lax.axis_index("sa")
    sb = lax.axis_index("sb")

    w_rows = lax.all_gather(o_weight, "sb", axis=0, tiled=True)
    kv_all = lax.all_gather(kv_pairs, ("sa", "sb"), axis=1, tiled=True)
    q_send = queries.reshape(tok_dev, n_sa, heads_here * head_size).transpose(1, 0, 2)
    q_rows = lax.all_to_all(q_send, "sa", split_axis=0, concat_axis=0, tiled=True)
    q_rows = q_rows.reshape(n_sa * tok_dev, heads_here * head_size)
    meta = jnp.stack([sb, (sa * heads_here) // sharing]).astype(jnp.int32)
    attended = attention(meta, q_rows, kv_all, heads_here, head_size, tok_dev, n_sb)

    partial_sum = None
    for j in range(w_rows.shape[0] // block_rows):
        cols = slice(j * block_rows, (j + 1) * block_rows)
        partial_j = jnp.dot(
            attended[:, cols], w_rows[cols], preferred_element_type=jnp.float32
        ).astype(jnp.bfloat16).astype(jnp.float32)
        partial_sum = partial_j if partial_sum is None else partial_sum + partial_j
    attn_out = lax.psum_scatter(
        partial_sum.astype(jnp.bfloat16), "sa", scatter_dimension=0, tiled=True
    ).astype(jnp.float32)
    mixed = residual.astype(jnp.float32) + attn_out
    mean_square = jnp.mean(mixed * mixed, axis=1, keepdims=True)
    normed = (mixed * lax.rsqrt(mean_square + 1e-06) * norm_gain.astype(jnp.float32)).astype(
        jnp.bfloat16
    )

    top_count = expert_ids.shape[1]
    capacity = 2 * tok_dev * top_count // devices
    slots = devices * capacity
    flat_ids = expert_ids.reshape(-1)
    flat_weights = route_weights.reshape(-1)
    n_flat = flat_ids.shape[0]
    onehot = (flat_ids[:, None] == jnp.arange(devices, dtype=jnp.int32)[None, :]).astype(
        jnp.bfloat16
    )
    row = lax.broadcasted_iota(jnp.int32, (n_flat, n_flat), 0)
    col = lax.broadcasted_iota(jnp.int32, (n_flat, n_flat), 1)
    before = (col < row).astype(jnp.bfloat16)
    earlier = jnp.dot(before, onehot, preferred_element_type=jnp.float32)
    rank = jnp.sum(earlier * onehot.astype(jnp.float32), axis=1).astype(jnp.int32)
    slot_index = flat_ids * capacity + rank
    picks = slot_index[:, None] == jnp.arange(slots, dtype=jnp.int32)[None, :]
    token_slots = jnp.any(picks.reshape(tok_dev, top_count, slots), axis=1).astype(jnp.bfloat16)
    outgoing_rows = lax.dot_general(
        token_slots, normed, (((0,), (0,)), ((), ())), preferred_element_type=jnp.float32
    ).astype(jnp.bfloat16)
    outgoing_rows = outgoing_rows.reshape(devices, capacity, width)
    ffe_width = w_down.shape[1]
    arrived = lax.all_to_all(outgoing_rows, ("grp", "sa", "sb"), split_axis=0, concat_axis=0, tiled=True)
    flat_rows = arrived.reshape(-1, width)
    projected = jnp.dot(flat_rows, w_in[0], preferred_element_type=jnp.float32)
    hidden = (jax.nn.silu(projected[:, :ffe_width]) * projected[:, ffe_width:]).astype(jnp.bfloat16)
    produced = jnp.dot(hidden, w_down[0], preferred_element_type=jnp.float32).astype(jnp.bfloat16)
    returned = lax.all_to_all(
        produced.reshape(arrived.shape), ("grp", "sa", "sb"), split_axis=0, concat_axis=0, tiled=True
    )
    returned = returned.reshape(slots, width)
    picks_by_choice = picks.reshape(tok_dev, top_count, slots).transpose(1, 0, 2)
    picked = jnp.dot(
        picks_by_choice.reshape(n_flat, slots).astype(jnp.bfloat16),
        returned,
        preferred_element_type=jnp.float32,
    ).reshape(top_count, tok_dev, width)
    weights_by_choice = route_weights.T.reshape(top_count, tok_dev, 1)
    combined = jnp.sum(picked * weights_by_choice, axis=0)
    return (mixed + combined).astype(jnp.bfloat16)


def solution(mesh):
    n_grp, n_seq = mesh.shape["grp"], mesh.shape["seq"]
    n_sb = math.isqrt(n_seq)
    grid = Mesh(mesh.devices.reshape(n_grp, n_seq // n_sb, n_sb), ("grp", "sa", "sb"))
    tokens = ("grp", "sa", "sb")
    return jax.shard_map(
        shards,
        mesh=grid,
        in_specs=(
            P(tokens, None),
            P(None, tokens, None),
            P(tokens, None),
            P(),
            P(("sa", "sb"), None),
            P(tokens, None, None),
            P(tokens, None, None),
            P(tokens, None),
            P(tokens, None),
        ),
        out_specs=P(tokens, None),
        check_vma=False,
    )
```

```python
import functools
import math

import jax
import jax.numpy as jnp
from jax import lax
from jax.experimental import pallas as pl
from jax.experimental.pallas import tpu as pltpu
from jax.sharding import Mesh, PartitionSpec as P

HD = 128
Q_BLOCK = 256


def _attend_kernel(meta_ref, q_ref, k_ref, v_ref, o_ref, *, block, scale, tok_dev, n_sb):
    qi = pl.program_id(1)
    sb = meta_ref[0]
    q = q_ref[...]
    k = k_ref[...]
    length = k.shape[0]
    scores = lax.dot_general(
        q, k, (((1,), (1,)), ((), ())), preferred_element_type=jnp.float32
    ) * scale
    local = qi * block + lax.broadcasted_iota(jnp.int32, (block, length), 0)
    q_pos = ((local // tok_dev) * n_sb + sb) * tok_dev + local % tok_dev
    k_pos = lax.broadcasted_iota(jnp.int32, (block, length), 1)
    scores = jnp.where(k_pos <= q_pos, scores, jnp.float32(-1e30))
    top = jnp.max(scores, axis=1, keepdims=True)
    weights = jnp.exp(scores - top)
    total = jnp.sum(weights, axis=1, keepdims=True)
    probs = (weights / total).astype(jnp.bfloat16)
    o_ref[...] = jnp.dot(probs, v_ref[...], preferred_element_type=jnp.float32).astype(
        o_ref.dtype
    )


def attention(meta, q_rows, kv_all, heads, head_size, tok_dev, n_sb):
    rows = q_rows.shape[0]
    seq_len = kv_all.shape[1]
    block = min(Q_BLOCK, rows)
    kernel = functools.partial(
        _attend_kernel, block=block, scale=1.0 / head_size**0.5, tok_dev=tok_dev, n_sb=n_sb
    )
    return pl.pallas_call(
        kernel,
        out_shape=jax.ShapeDtypeStruct((rows, heads * head_size), jnp.bfloat16),
        grid_spec=pltpu.PrefetchScalarGridSpec(
            num_scalar_prefetch=1,
            grid=(heads, rows // block),
            in_specs=[
                pl.BlockSpec((block, head_size), lambda h, i, m: (i, h)),
                pl.BlockSpec((None, seq_len, head_size), lambda h, i, m: (0, 0, m[1])),
                pl.BlockSpec((None, seq_len, head_size), lambda h, i, m: (1, 0, m[1])),
            ],
            out_specs=pl.BlockSpec((block, head_size), lambda h, i, m: (i, h)),
        ),
        compiler_params=pltpu.CompilerParams(
            dimension_semantics=("arbitrary", "arbitrary"),
            vmem_limit_bytes=48 * 1024 * 1024,
        ),
    )(meta, q_rows, kv_all, kv_all)


def shards(
    queries, kv_pairs, residual, norm_gain, o_weight, w_in, w_down, expert_ids, route_weights
):
    tok_dev = queries.shape[0]
    width = residual.shape[1]
    n_sa = lax.axis_size("sa")
    n_sb = lax.axis_size("sb")
    n_seq = n_sa * n_sb
    n_grp = lax.axis_size("grp")
    devices = n_seq * n_grp
    head_size = HD
    heads_all = queries.shape[1] // head_size
    key_heads = kv_pairs.shape[2] // head_size
    sharing = heads_all // key_heads
    heads_here = heads_all // n_sa
    block_rows = o_weight.shape[0]
    assert sharing % heads_here == 0
    sa = lax.axis_index("sa")
    sb = lax.axis_index("sb")

    pair = lax.axis_index("grp") % 2
    half = o_weight.shape[1] // 2
    w_mine = lax.all_gather(
        lax.dynamic_slice_in_dim(o_weight, pair * half, half, axis=1), "sb", axis=0, tiled=True
    )
    w_other = lax.ppermute(w_mine, "grp", [(g, g ^ 1) for g in range(n_grp)])
    w_rows = jnp.zeros((w_mine.shape[0], 2 * half), o_weight.dtype)
    w_rows = lax.dynamic_update_slice_in_dim(w_rows, w_mine, pair * half, axis=1)
    w_rows = lax.dynamic_update_slice_in_dim(w_rows, w_other, (1 - pair) * half, axis=1)
    kv_all = lax.all_gather(kv_pairs, ("sa", "sb"), axis=1, tiled=True)
    q_send = queries.reshape(tok_dev, n_sa, heads_here * head_size).transpose(1, 0, 2)
    q_rows = lax.all_to_all(q_send, "sa", split_axis=0, concat_axis=0, tiled=True)
    q_rows = q_rows.reshape(n_sa * tok_dev, heads_here * head_size)
    meta = jnp.stack([sb, (sa * heads_here) // sharing]).astype(jnp.int32)
    attended = attention(meta, q_rows, kv_all, heads_here, head_size, tok_dev, n_sb)

    partial_sum = None
    for j in range(w_rows.shape[0] // block_rows):
        cols = slice(j * block_rows, (j + 1) * block_rows)
        partial_j = jnp.dot(
            attended[:, cols], w_rows[cols], preferred_element_type=jnp.float32
        ).astype(jnp.bfloat16).astype(jnp.float32)
        partial_sum = partial_j if partial_sum is None else partial_sum + partial_j
    attn_out = lax.psum_scatter(
        partial_sum.astype(jnp.bfloat16), "sa", scatter_dimension=0, tiled=True
    ).astype(jnp.float32)
    mixed = residual.astype(jnp.float32) + attn_out
    mean_square = jnp.mean(mixed * mixed, axis=1, keepdims=True)
    normed = (mixed * lax.rsqrt(mean_square + 1e-06) * norm_gain.astype(jnp.float32)).astype(
        jnp.bfloat16
    )

    top_count = expert_ids.shape[1]
    capacity = 2 * tok_dev * top_count // devices
    slots = devices * capacity
    flat_ids = expert_ids.reshape(-1)
    flat_weights = route_weights.reshape(-1)
    n_flat = flat_ids.shape[0]
    onehot = (flat_ids[:, None] == jnp.arange(devices, dtype=jnp.int32)[None, :]).astype(
        jnp.bfloat16
    )
    row = lax.broadcasted_iota(jnp.int32, (n_flat, n_flat), 0)
    col = lax.broadcasted_iota(jnp.int32, (n_flat, n_flat), 1)
    before = (col < row).astype(jnp.bfloat16)
    earlier = jnp.dot(before, onehot, preferred_element_type=jnp.float32)
    rank = jnp.sum(earlier * onehot.astype(jnp.float32), axis=1).astype(jnp.int32)
    slot_index = flat_ids * capacity + rank
    picks = slot_index[:, None] == jnp.arange(slots, dtype=jnp.int32)[None, :]
    token_slots = jnp.any(picks.reshape(tok_dev, top_count, slots), axis=1).astype(jnp.bfloat16)
    outgoing_rows = lax.dot_general(
        token_slots, normed, (((0,), (0,)), ((), ())), preferred_element_type=jnp.float32
    ).astype(jnp.bfloat16)
    outgoing_rows = outgoing_rows.reshape(devices, capacity, width)
    ffe_width = w_down.shape[1]
    arrived = lax.all_to_all(outgoing_rows, ("grp", "sa", "sb"), split_axis=0, concat_axis=0, tiled=True)
    flat_rows = arrived.reshape(-1, width)
    projected = jnp.dot(flat_rows, w_in[0], preferred_element_type=jnp.float32)
    hidden = (jax.nn.silu(projected[:, :ffe_width]) * projected[:, ffe_width:]).astype(jnp.bfloat16)
    produced = jnp.dot(hidden, w_down[0], preferred_element_type=jnp.float32).astype(jnp.bfloat16)
    returned = lax.all_to_all(
        produced.reshape(arrived.shape), ("grp", "sa", "sb"), split_axis=0, concat_axis=0, tiled=True
    )
    returned = returned.reshape(slots, width)
    picks_by_choice = picks.reshape(tok_dev, top_count, slots).transpose(1, 0, 2)
    picked = jnp.dot(
        picks_by_choice.reshape(n_flat, slots).astype(jnp.bfloat16),
        returned,
        preferred_element_type=jnp.float32,
    ).reshape(top_count, tok_dev, width)
    weights_by_choice = route_weights.T.reshape(top_count, tok_dev, 1)
    combined = jnp.sum(picked * weights_by_choice, axis=0)
    return (mixed + combined).astype(jnp.bfloat16)


def solution(mesh):
    n_grp, n_seq = mesh.shape["grp"], mesh.shape["seq"]
    n_sb = math.isqrt(n_seq)
    grid = Mesh(mesh.devices.reshape(n_grp, n_seq // n_sb, n_sb), ("grp", "sa", "sb"))
    tokens = ("grp", "sa", "sb")
    return jax.shard_map(
        shards,
        mesh=grid,
        in_specs=(
            P(tokens, None),
            P(None, tokens, None),
            P(tokens, None),
            P(),
            P(("sa", "sb"), None),
            P(tokens, None, None),
            P(tokens, None, None),
            P(tokens, None),
            P(tokens, None),
        ),
        out_specs=P(tokens, None),
        check_vma=False,
    )
```

```python
import functools
import math

import jax
import jax.numpy as jnp
from jax import lax
from jax.experimental import pallas as pl
from jax.experimental.pallas import tpu as pltpu
from jax.sharding import Mesh, PartitionSpec as P

HD = 128
Q_BLOCK = 256


def _attend_kernel(meta_ref, q_ref, k_ref, v_ref, o_ref, *, block, scale, tok_dev, n_sb):
    qi = pl.program_id(1)
    sb = meta_ref[0]
    q = q_ref[...]
    k = k_ref[...]
    length = k.shape[0]
    scores = lax.dot_general(
        q, k, (((1,), (1,)), ((), ())), preferred_element_type=jnp.float32
    ) * scale
    local = qi * block + lax.broadcasted_iota(jnp.int32, (block, length), 0)
    q_pos = ((local // tok_dev) * n_sb + sb) * tok_dev + local % tok_dev
    k_pos = lax.broadcasted_iota(jnp.int32, (block, length), 1)
    scores = jnp.where(k_pos <= q_pos, scores, jnp.float32(-1e30))
    top = jnp.max(scores, axis=1, keepdims=True)
    weights = jnp.exp(scores - top)
    total = jnp.sum(weights, axis=1, keepdims=True)
    probs = (weights / total).astype(jnp.bfloat16)
    o_ref[...] = jnp.dot(probs, v_ref[...], preferred_element_type=jnp.float32).astype(
        o_ref.dtype
    )


def attention(meta, q_rows, kv_all, heads, head_size, tok_dev, n_sb):
    rows = q_rows.shape[0]
    seq_len = kv_all.shape[1]
    block = min(Q_BLOCK, rows)
    kernel = functools.partial(
        _attend_kernel, block=block, scale=1.0 / head_size**0.5, tok_dev=tok_dev, n_sb=n_sb
    )
    return pl.pallas_call(
        kernel,
        out_shape=jax.ShapeDtypeStruct((rows, heads * head_size), jnp.bfloat16),
        grid_spec=pltpu.PrefetchScalarGridSpec(
            num_scalar_prefetch=1,
            grid=(heads, rows // block),
            in_specs=[
                pl.BlockSpec((block, head_size), lambda h, i, m: (i, h)),
                pl.BlockSpec((None, seq_len, head_size), lambda h, i, m: (0, 0, m[1])),
                pl.BlockSpec((None, seq_len, head_size), lambda h, i, m: (1, 0, m[1])),
            ],
            out_specs=pl.BlockSpec((block, head_size), lambda h, i, m: (i, h)),
        ),
        compiler_params=pltpu.CompilerParams(
            dimension_semantics=("arbitrary", "arbitrary"),
            vmem_limit_bytes=48 * 1024 * 1024,
        ),
    )(meta, q_rows, kv_all, kv_all)


def shards(
    queries, kv_pairs, residual, norm_gain, o_weight, w_in, w_down, expert_ids, route_weights
):
    tok_dev = queries.shape[0]
    width = residual.shape[1]
    n_sa = lax.axis_size("sa")
    n_sb = lax.axis_size("sb")
    n_seq = n_sa * n_sb
    n_grp = lax.axis_size("grp")
    devices = n_seq * n_grp
    head_size = HD
    heads_all = queries.shape[1] // head_size
    key_heads = kv_pairs.shape[2] // head_size
    sharing = heads_all // key_heads
    heads_here = heads_all // n_sa
    block_rows = o_weight.shape[0]
    assert sharing % heads_here == 0
    sa = lax.axis_index("sa")
    sb = lax.axis_index("sb")

    pair = lax.axis_index("grp") % 2
    half = o_weight.shape[1] // 2
    own = lax.dynamic_slice_in_dim(o_weight, pair * half, half, axis=1)
    block_rows = o_weight.shape[0]
    pieces = {0: own}
    for step_dir, count in ((1, n_sb // 2), (-1, (n_sb - 1) // 2)):
        ring = [(i, (i + step_dir) % n_sb) for i in range(n_sb)]
        held = own
        for k in range(1, count + 1):
            held = lax.ppermute(held, "sb", ring)
            pieces[-step_dir * k] = held
    w_mine = jnp.zeros((n_sb * block_rows, half), o_weight.dtype)
    for offset, piece in pieces.items():
        w_mine = lax.dynamic_update_slice_in_dim(
            w_mine, piece, ((sb + offset) % n_sb) * block_rows, axis=0
        )
    w_other = lax.ppermute(w_mine, "grp", [(g, g ^ 1) for g in range(n_grp)])
    w_rows = jnp.zeros((w_mine.shape[0], 2 * half), o_weight.dtype)
    w_rows = lax.dynamic_update_slice_in_dim(w_rows, w_mine, pair * half, axis=1)
    w_rows = lax.dynamic_update_slice_in_dim(w_rows, w_other, (1 - pair) * half, axis=1)
    kv_all = lax.all_gather(kv_pairs, ("sa", "sb"), axis=1, tiled=True)
    q_send = queries.reshape(tok_dev, n_sa, heads_here * head_size).transpose(1, 0, 2)
    q_rows = lax.all_to_all(q_send, "sa", split_axis=0, concat_axis=0, tiled=True)
    q_rows = q_rows.reshape(n_sa * tok_dev, heads_here * head_size)
    meta = jnp.stack([sb, (sa * heads_here) // sharing]).astype(jnp.int32)
    attended = attention(meta, q_rows, kv_all, heads_here, head_size, tok_dev, n_sb)

    partial_sum = None
    for j in range(w_rows.shape[0] // block_rows):
        cols = slice(j * block_rows, (j + 1) * block_rows)
        partial_j = jnp.dot(
            attended[:, cols], w_rows[cols], preferred_element_type=jnp.float32
        ).astype(jnp.bfloat16).astype(jnp.float32)
        partial_sum = partial_j if partial_sum is None else partial_sum + partial_j
    attn_out = lax.psum_scatter(
        partial_sum.astype(jnp.bfloat16), "sa", scatter_dimension=0, tiled=True
    ).astype(jnp.float32)
    mixed = residual.astype(jnp.float32) + attn_out
    mean_square = jnp.mean(mixed * mixed, axis=1, keepdims=True)
    normed = (mixed * lax.rsqrt(mean_square + 1e-06) * norm_gain.astype(jnp.float32)).astype(
        jnp.bfloat16
    )

    top_count = expert_ids.shape[1]
    capacity = 2 * tok_dev * top_count // devices
    slots = devices * capacity
    flat_ids = expert_ids.reshape(-1)
    flat_weights = route_weights.reshape(-1)
    n_flat = flat_ids.shape[0]
    onehot = (flat_ids[:, None] == jnp.arange(devices, dtype=jnp.int32)[None, :]).astype(
        jnp.bfloat16
    )
    row = lax.broadcasted_iota(jnp.int32, (n_flat, n_flat), 0)
    col = lax.broadcasted_iota(jnp.int32, (n_flat, n_flat), 1)
    before = (col < row).astype(jnp.bfloat16)
    earlier = jnp.dot(before, onehot, preferred_element_type=jnp.float32)
    rank = jnp.sum(earlier * onehot.astype(jnp.float32), axis=1).astype(jnp.int32)
    slot_index = flat_ids * capacity + rank
    picks = slot_index[:, None] == jnp.arange(slots, dtype=jnp.int32)[None, :]
    token_slots = jnp.any(picks.reshape(tok_dev, top_count, slots), axis=1).astype(jnp.bfloat16)
    outgoing_rows = lax.dot_general(
        token_slots, normed, (((0,), (0,)), ((), ())), preferred_element_type=jnp.float32
    ).astype(jnp.bfloat16)
    outgoing_rows = outgoing_rows.reshape(devices, capacity, width)
    ffe_width = w_down.shape[1]
    arrived = lax.all_to_all(outgoing_rows, ("grp", "sa", "sb"), split_axis=0, concat_axis=0, tiled=True)
    flat_rows = arrived.reshape(-1, width)
    projected = jnp.dot(flat_rows, w_in[0], preferred_element_type=jnp.float32)
    hidden = (jax.nn.silu(projected[:, :ffe_width]) * projected[:, ffe_width:]).astype(jnp.bfloat16)
    produced = jnp.dot(hidden, w_down[0], preferred_element_type=jnp.float32).astype(jnp.bfloat16)
    returned = lax.all_to_all(
        produced.reshape(arrived.shape), ("grp", "sa", "sb"), split_axis=0, concat_axis=0, tiled=True
    )
    returned = returned.reshape(slots, width)
    picks_by_choice = picks.reshape(tok_dev, top_count, slots).transpose(1, 0, 2)
    picked = jnp.dot(
        picks_by_choice.reshape(n_flat, slots).astype(jnp.bfloat16),
        returned,
        preferred_element_type=jnp.float32,
    ).reshape(top_count, tok_dev, width)
    weights_by_choice = route_weights.T.reshape(top_count, tok_dev, 1)
    combined = jnp.sum(picked * weights_by_choice, axis=0)
    return (mixed + combined).astype(jnp.bfloat16)


def solution(mesh):
    n_grp, n_seq = mesh.shape["grp"], mesh.shape["seq"]
    n_sb = math.isqrt(n_seq)
    grid = Mesh(mesh.devices.reshape(n_grp, n_seq // n_sb, n_sb), ("grp", "sa", "sb"))
    tokens = ("grp", "sa", "sb")
    return jax.shard_map(
        shards,
        mesh=grid,
        in_specs=(
            P(tokens, None),
            P(None, tokens, None),
            P(tokens, None),
            P(),
            P(("sa", "sb"), None),
            P(tokens, None, None),
            P(tokens, None, None),
            P(tokens, None),
            P(tokens, None),
        ),
        out_specs=P(tokens, None),
        check_vma=False,
    )
```

```python
import functools
import math

import jax
import jax.numpy as jnp
from jax import lax
from jax.experimental import pallas as pl
from jax.experimental.pallas import tpu as pltpu
from jax.sharding import Mesh, PartitionSpec as P

HD = 128
Q_BLOCK = 256


def _attend_kernel(meta_ref, q_ref, k_ref, v_ref, o_ref, *, block, scale, tok_dev, n_sb):
    qi = pl.program_id(1)
    sb = meta_ref[0]
    q = q_ref[...]
    k = k_ref[...]
    length = k.shape[0]
    scores = lax.dot_general(
        q, k, (((1,), (1,)), ((), ())), preferred_element_type=jnp.float32
    ) * scale
    local = qi * block + lax.broadcasted_iota(jnp.int32, (block, length), 0)
    q_pos = ((local // tok_dev) * n_sb + sb) * tok_dev + local % tok_dev
    k_pos = lax.broadcasted_iota(jnp.int32, (block, length), 1)
    scores = jnp.where(k_pos <= q_pos, scores, jnp.float32(-1e30))
    top = jnp.max(scores, axis=1, keepdims=True)
    weights = jnp.exp(scores - top)
    total = jnp.sum(weights, axis=1, keepdims=True)
    probs = (weights / total).astype(jnp.bfloat16)
    o_ref[...] = jnp.dot(probs, v_ref[...], preferred_element_type=jnp.float32).astype(
        o_ref.dtype
    )


def attention(meta, q_rows, kv_all, heads, head_size, tok_dev, n_sb):
    rows = q_rows.shape[0]
    seq_len = kv_all.shape[1]
    block = min(Q_BLOCK, rows)
    kernel = functools.partial(
        _attend_kernel, block=block, scale=1.0 / head_size**0.5, tok_dev=tok_dev, n_sb=n_sb
    )
    return pl.pallas_call(
        kernel,
        out_shape=jax.ShapeDtypeStruct((rows, heads * head_size), jnp.bfloat16),
        grid_spec=pltpu.PrefetchScalarGridSpec(
            num_scalar_prefetch=1,
            grid=(heads, rows // block),
            in_specs=[
                pl.BlockSpec((block, head_size), lambda h, i, m: (i, h)),
                pl.BlockSpec((None, seq_len, head_size), lambda h, i, m: (0, 0, m[1])),
                pl.BlockSpec((None, seq_len, head_size), lambda h, i, m: (1, 0, m[1])),
            ],
            out_specs=pl.BlockSpec((block, head_size), lambda h, i, m: (i, h)),
        ),
        compiler_params=pltpu.CompilerParams(
            dimension_semantics=("arbitrary", "arbitrary"),
            vmem_limit_bytes=48 * 1024 * 1024,
        ),
    )(meta, q_rows, kv_all, kv_all)


def shards(
    queries, kv_pairs, residual, norm_gain, o_weight, w_in, w_down, expert_ids, route_weights
):
    tok_dev = queries.shape[0]
    width = residual.shape[1]
    n_sa = lax.axis_size("sa")
    n_sb = lax.axis_size("sb")
    n_seq = n_sa * n_sb
    n_grp = lax.axis_size("grp")
    devices = n_seq * n_grp
    head_size = HD
    heads_all = queries.shape[1] // head_size
    key_heads = kv_pairs.shape[2] // head_size
    sharing = heads_all // key_heads
    heads_here = heads_all // n_sa
    block_rows = o_weight.shape[0]
    assert sharing % heads_here == 0
    sa = lax.axis_index("sa")
    sb = lax.axis_index("sb")

    pair = lax.axis_index("grp") % 2
    half = o_weight.shape[1] // 2
    own = lax.dynamic_slice_in_dim(o_weight, pair * half, half, axis=1)
    w_mine = lax.all_to_all(
        jnp.broadcast_to(own[None], (n_sb,) + own.shape), "sb", split_axis=0, concat_axis=0,
        tiled=True,
    ).reshape(n_sb * own.shape[0], half)
    w_other = lax.ppermute(w_mine, "grp", [(g, g ^ 1) for g in range(n_grp)])
    w_rows = jnp.zeros((w_mine.shape[0], 2 * half), o_weight.dtype)
    w_rows = lax.dynamic_update_slice_in_dim(w_rows, w_mine, pair * half, axis=1)
    w_rows = lax.dynamic_update_slice_in_dim(w_rows, w_other, (1 - pair) * half, axis=1)
    kv_all = lax.all_gather(kv_pairs, ("sa", "sb"), axis=1, tiled=True)
    q_send = queries.reshape(tok_dev, n_sa, heads_here * head_size).transpose(1, 0, 2)
    q_rows = lax.all_to_all(q_send, "sa", split_axis=0, concat_axis=0, tiled=True)
    q_rows = q_rows.reshape(n_sa * tok_dev, heads_here * head_size)
    meta = jnp.stack([sb, (sa * heads_here) // sharing]).astype(jnp.int32)
    attended = attention(meta, q_rows, kv_all, heads_here, head_size, tok_dev, n_sb)

    partial_sum = None
    for j in range(w_rows.shape[0] // block_rows):
        cols = slice(j * block_rows, (j + 1) * block_rows)
        partial_j = jnp.dot(
            attended[:, cols], w_rows[cols], preferred_element_type=jnp.float32
        ).astype(jnp.bfloat16).astype(jnp.float32)
        partial_sum = partial_j if partial_sum is None else partial_sum + partial_j
    attn_out = lax.psum_scatter(
        partial_sum.astype(jnp.bfloat16), "sa", scatter_dimension=0, tiled=True
    ).astype(jnp.float32)
    mixed = residual.astype(jnp.float32) + attn_out
    mean_square = jnp.mean(mixed * mixed, axis=1, keepdims=True)
    normed = (mixed * lax.rsqrt(mean_square + 1e-06) * norm_gain.astype(jnp.float32)).astype(
        jnp.bfloat16
    )

    top_count = expert_ids.shape[1]
    capacity = 2 * tok_dev * top_count // devices
    slots = devices * capacity
    flat_ids = expert_ids.reshape(-1)
    flat_weights = route_weights.reshape(-1)
    n_flat = flat_ids.shape[0]
    onehot = (flat_ids[:, None] == jnp.arange(devices, dtype=jnp.int32)[None, :]).astype(
        jnp.bfloat16
    )
    row = lax.broadcasted_iota(jnp.int32, (n_flat, n_flat), 0)
    col = lax.broadcasted_iota(jnp.int32, (n_flat, n_flat), 1)
    before = (col < row).astype(jnp.bfloat16)
    earlier = jnp.dot(before, onehot, preferred_element_type=jnp.float32)
    rank = jnp.sum(earlier * onehot.astype(jnp.float32), axis=1).astype(jnp.int32)
    slot_index = flat_ids * capacity + rank
    picks = slot_index[:, None] == jnp.arange(slots, dtype=jnp.int32)[None, :]
    token_slots = jnp.any(picks.reshape(tok_dev, top_count, slots), axis=1).astype(jnp.bfloat16)
    outgoing_rows = lax.dot_general(
        token_slots, normed, (((0,), (0,)), ((), ())), preferred_element_type=jnp.float32
    ).astype(jnp.bfloat16)
    outgoing_rows = outgoing_rows.reshape(devices, capacity, width)
    ffe_width = w_down.shape[1]
    arrived = lax.all_to_all(outgoing_rows, ("grp", "sa", "sb"), split_axis=0, concat_axis=0, tiled=True)
    flat_rows = arrived.reshape(-1, width)
    projected = jnp.dot(flat_rows, w_in[0], preferred_element_type=jnp.float32)
    hidden = (jax.nn.silu(projected[:, :ffe_width]) * projected[:, ffe_width:]).astype(jnp.bfloat16)
    produced = jnp.dot(hidden, w_down[0], preferred_element_type=jnp.float32).astype(jnp.bfloat16)
    returned = lax.all_to_all(
        produced.reshape(arrived.shape), ("grp", "sa", "sb"), split_axis=0, concat_axis=0, tiled=True
    )
    returned = returned.reshape(slots, width)
    picks_by_choice = picks.reshape(tok_dev, top_count, slots).transpose(1, 0, 2)
    picked = jnp.dot(
        picks_by_choice.reshape(n_flat, slots).astype(jnp.bfloat16),
        returned,
        preferred_element_type=jnp.float32,
    ).reshape(top_count, tok_dev, width)
    weights_by_choice = route_weights.T.reshape(top_count, tok_dev, 1)
    combined = jnp.sum(picked * weights_by_choice, axis=0)
    return (mixed + combined).astype(jnp.bfloat16)


def solution(mesh):
    n_grp, n_seq = mesh.shape["grp"], mesh.shape["seq"]
    n_sb = math.isqrt(n_seq)
    grid = Mesh(mesh.devices.reshape(n_grp, n_seq // n_sb, n_sb), ("grp", "sa", "sb"))
    tokens = ("grp", "sa", "sb")
    return jax.shard_map(
        shards,
        mesh=grid,
        in_specs=(
            P(tokens, None),
            P(None, tokens, None),
            P(tokens, None),
            P(),
            P(("sa", "sb"), None),
            P(tokens, None, None),
            P(tokens, None, None),
            P(tokens, None),
            P(tokens, None),
        ),
        out_specs=P(tokens, None),
        check_vma=False,
    )
```

```python
import functools
import math

import jax
import jax.numpy as jnp
from jax import lax
from jax.experimental import pallas as pl
from jax.experimental.pallas import tpu as pltpu
from jax.sharding import Mesh, PartitionSpec as P

HD = 128
Q_BLOCK = 256


def _attend_kernel(meta_ref, q_ref, k_ref, v_ref, o_ref, *, block, scale, tok_dev, n_sb):
    qi = pl.program_id(1)
    sb = meta_ref[0]
    q = q_ref[...]
    k = k_ref[...]
    length = k.shape[0]
    scores = lax.dot_general(
        q, k, (((1,), (1,)), ((), ())), preferred_element_type=jnp.float32
    ) * scale
    local = qi * block + lax.broadcasted_iota(jnp.int32, (block, length), 0)
    q_pos = ((local // tok_dev) * n_sb + sb) * tok_dev + local % tok_dev
    k_pos = lax.broadcasted_iota(jnp.int32, (block, length), 1)
    scores = jnp.where(k_pos <= q_pos, scores, jnp.float32(-1e30))
    top = jnp.max(scores, axis=1, keepdims=True)
    weights = jnp.exp(scores - top)
    total = jnp.sum(weights, axis=1, keepdims=True)
    probs = (weights / total).astype(jnp.bfloat16)
    o_ref[...] = jnp.dot(probs, v_ref[...], preferred_element_type=jnp.float32).astype(
        o_ref.dtype
    )


def attention(meta, q_rows, kv_all, heads, head_size, tok_dev, n_sb):
    rows = q_rows.shape[0]
    seq_len = kv_all.shape[0]
    block = min(Q_BLOCK, rows)
    kernel = functools.partial(
        _attend_kernel, block=block, scale=1.0 / head_size**0.5, tok_dev=tok_dev, n_sb=n_sb
    )
    return pl.pallas_call(
        kernel,
        out_shape=jax.ShapeDtypeStruct((rows, heads * head_size), jnp.bfloat16),
        grid_spec=pltpu.PrefetchScalarGridSpec(
            num_scalar_prefetch=1,
            grid=(heads, rows // block),
            in_specs=[
                pl.BlockSpec((block, head_size), lambda h, i, m: (i, h)),
                pl.BlockSpec((seq_len, head_size), lambda h, i, m: (0, 0)),
                pl.BlockSpec((seq_len, head_size), lambda h, i, m: (0, 1)),
            ],
            out_specs=pl.BlockSpec((block, head_size), lambda h, i, m: (i, h)),
        ),
        compiler_params=pltpu.CompilerParams(
            dimension_semantics=("arbitrary", "arbitrary"),
            vmem_limit_bytes=48 * 1024 * 1024,
        ),
    )(meta, q_rows, kv_all, kv_all)


def shards(
    queries, kv_pairs, residual, norm_gain, o_weight, w_in, w_down, expert_ids, route_weights
):
    tok_dev = queries.shape[0]
    width = residual.shape[1]
    n_sa = lax.axis_size("sa")
    n_sb = lax.axis_size("sb")
    n_seq = n_sa * n_sb
    n_grp = lax.axis_size("grp")
    devices = n_seq * n_grp
    head_size = HD
    heads_all = queries.shape[1] // head_size
    key_heads = kv_pairs.shape[2] // head_size
    sharing = heads_all // key_heads
    heads_here = heads_all // n_sa
    block_rows = o_weight.shape[0]
    assert sharing % heads_here == 0
    sa = lax.axis_index("sa")
    sb = lax.axis_index("sb")

    pair = lax.axis_index("grp") % 2
    half = o_weight.shape[1] // 2
    w_mine = lax.all_gather(
        lax.dynamic_slice_in_dim(o_weight, pair * half, half, axis=1), "sb", axis=0, tiled=True
    )
    q_send = queries.reshape(tok_dev, n_sa, heads_here * head_size).transpose(1, 0, 2)
    kv_heads = kv_pairs.reshape(2, tok_dev, key_heads, head_size)
    head_of_dest = (jnp.arange(n_sa) * heads_here) // sharing
    kv_send = jnp.take(kv_heads, head_of_dest, axis=2)
    kv_send = kv_send.transpose(2, 1, 0, 3).reshape(n_sa, tok_dev, 2 * head_size)
    packed = lax.all_to_all(
        jnp.concatenate([q_send, kv_send], axis=2), "sa", split_axis=0, concat_axis=0, tiled=True
    )
    q_rows = packed[:, :, : heads_here * head_size].reshape(n_sa * tok_dev, heads_here * head_size)
    kv_col = packed[:, :, heads_here * head_size :]
    kv_grid = lax.all_to_all(
        jnp.broadcast_to(kv_col[None], (n_sb,) + kv_col.shape), "sb", split_axis=0,
        concat_axis=0, tiled=True,
    )
    kv_all = kv_grid.transpose(1, 0, 2, 3).reshape(n_seq * tok_dev, 2 * head_size)
    meta = jnp.stack([sb, jnp.zeros_like(sb)]).astype(jnp.int32)
    attended = attention(meta, q_rows, kv_all, heads_here, head_size, tok_dev, n_sb)

    w_mine, attended = lax.optimization_barrier((w_mine, attended))
    w_other = lax.ppermute(w_mine, "grp", [(g, g ^ 1) for g in range(n_grp)])
    w_rows = jnp.zeros((w_mine.shape[0], 2 * half), o_weight.dtype)
    w_rows = lax.dynamic_update_slice_in_dim(w_rows, w_mine, pair * half, axis=1)
    w_rows = lax.dynamic_update_slice_in_dim(w_rows, w_other, (1 - pair) * half, axis=1)

    partial_sum = None
    for j in range(w_rows.shape[0] // block_rows):
        cols = slice(j * block_rows, (j + 1) * block_rows)
        partial_j = jnp.dot(
            attended[:, cols], w_rows[cols], preferred_element_type=jnp.float32
        ).astype(jnp.bfloat16).astype(jnp.float32)
        partial_sum = partial_j if partial_sum is None else partial_sum + partial_j
    attn_out = lax.psum_scatter(
        partial_sum.astype(jnp.bfloat16), "sa", scatter_dimension=0, tiled=True
    ).astype(jnp.float32)
    mixed = residual.astype(jnp.float32) + attn_out
    mean_square = jnp.mean(mixed * mixed, axis=1, keepdims=True)
    normed = (mixed * lax.rsqrt(mean_square + 1e-06) * norm_gain.astype(jnp.float32)).astype(
        jnp.bfloat16
    )

    top_count = expert_ids.shape[1]
    capacity = 2 * tok_dev * top_count // devices
    slots = devices * capacity
    flat_ids = expert_ids.reshape(-1)
    flat_weights = route_weights.reshape(-1)
    n_flat = flat_ids.shape[0]
    onehot = (flat_ids[:, None] == jnp.arange(devices, dtype=jnp.int32)[None, :]).astype(
        jnp.bfloat16
    )
    row = lax.broadcasted_iota(jnp.int32, (n_flat, n_flat), 0)
    col = lax.broadcasted_iota(jnp.int32, (n_flat, n_flat), 1)
    before = (col < row).astype(jnp.bfloat16)
    earlier = jnp.dot(before, onehot, preferred_element_type=jnp.float32)
    rank = jnp.sum(earlier * onehot.astype(jnp.float32), axis=1).astype(jnp.int32)
    slot_index = flat_ids * capacity + rank
    picks = slot_index[:, None] == jnp.arange(slots, dtype=jnp.int32)[None, :]
    token_slots = jnp.any(picks.reshape(tok_dev, top_count, slots), axis=1).astype(jnp.bfloat16)
    outgoing_rows = lax.dot_general(
        token_slots, normed, (((0,), (0,)), ((), ())), preferred_element_type=jnp.float32
    ).astype(jnp.bfloat16)
    outgoing_rows = outgoing_rows.reshape(devices, capacity, width)
    ffe_width = w_down.shape[1]
    arrived = lax.all_to_all(outgoing_rows, ("grp", "sa", "sb"), split_axis=0, concat_axis=0, tiled=True)
    flat_rows = arrived.reshape(-1, width)
    projected = jnp.dot(flat_rows, w_in[0], preferred_element_type=jnp.float32)
    hidden = (jax.nn.silu(projected[:, :ffe_width]) * projected[:, ffe_width:]).astype(jnp.bfloat16)
    produced = jnp.dot(hidden, w_down[0], preferred_element_type=jnp.float32).astype(jnp.bfloat16)
    returned = lax.all_to_all(
        produced.reshape(arrived.shape), ("grp", "sa", "sb"), split_axis=0, concat_axis=0, tiled=True
    )
    returned = returned.reshape(slots, width)
    picks_by_choice = picks.reshape(tok_dev, top_count, slots).transpose(1, 0, 2)
    picked = jnp.dot(
        picks_by_choice.reshape(n_flat, slots).astype(jnp.bfloat16),
        returned,
        preferred_element_type=jnp.float32,
    ).reshape(top_count, tok_dev, width)
    weights_by_choice = route_weights.T.reshape(top_count, tok_dev, 1)
    combined = jnp.sum(picked * weights_by_choice, axis=0)
    return (mixed + combined).astype(jnp.bfloat16)


def solution(mesh):
    n_grp, n_seq = mesh.shape["grp"], mesh.shape["seq"]
    n_sb = math.isqrt(n_seq)
    grid = Mesh(mesh.devices.reshape(n_grp, n_seq // n_sb, n_sb), ("grp", "sa", "sb"))
    tokens = ("grp", "sa", "sb")
    return jax.shard_map(
        shards,
        mesh=grid,
        in_specs=(
            P(tokens, None),
            P(None, tokens, None),
            P(tokens, None),
            P(),
            P(("sa", "sb"), None),
            P(tokens, None, None),
            P(tokens, None, None),
            P(tokens, None),
            P(tokens, None),
        ),
        out_specs=P(tokens, None),
        check_vma=False,
    )
```

```python
import functools
import math

import jax
import jax.numpy as jnp
from jax import lax
from jax.experimental import pallas as pl
from jax.experimental.pallas import tpu as pltpu
from jax.sharding import Mesh, PartitionSpec as P

HD = 128
Q_BLOCK = 256


def _attend_kernel(meta_ref, q_ref, k_ref, v_ref, o_ref, *, block, scale, tok_dev, n_sb):
    qi = pl.program_id(1)
    sb = meta_ref[0]
    q = q_ref[...]
    k = k_ref[...]
    length = k.shape[0]
    scores = lax.dot_general(
        q, k, (((1,), (1,)), ((), ())), preferred_element_type=jnp.float32
    ) * scale
    local = qi * block + lax.broadcasted_iota(jnp.int32, (block, length), 0)
    q_pos = ((local // tok_dev) * n_sb + sb) * tok_dev + local % tok_dev
    k_pos = lax.broadcasted_iota(jnp.int32, (block, length), 1)
    scores = jnp.where(k_pos <= q_pos, scores, jnp.float32(-1e30))
    top = jnp.max(scores, axis=1, keepdims=True)
    weights = jnp.exp(scores - top)
    total = jnp.sum(weights, axis=1, keepdims=True)
    probs = (weights / total).astype(jnp.bfloat16)
    o_ref[...] = jnp.dot(probs, v_ref[...], preferred_element_type=jnp.float32).astype(
        o_ref.dtype
    )


def attention(meta, q_rows, kv_all, heads, head_size, tok_dev, n_sb):
    rows = q_rows.shape[0]
    seq_len = kv_all.shape[0]
    block = min(Q_BLOCK, rows)
    kernel = functools.partial(
        _attend_kernel, block=block, scale=1.0 / head_size**0.5, tok_dev=tok_dev, n_sb=n_sb
    )
    return pl.pallas_call(
        kernel,
        out_shape=jax.ShapeDtypeStruct((rows, heads * head_size), jnp.bfloat16),
        grid_spec=pltpu.PrefetchScalarGridSpec(
            num_scalar_prefetch=1,
            grid=(heads, rows // block),
            in_specs=[
                pl.BlockSpec((block, head_size), lambda h, i, m: (i, h)),
                pl.BlockSpec((seq_len, head_size), lambda h, i, m: (0, 0)),
                pl.BlockSpec((seq_len, head_size), lambda h, i, m: (0, 1)),
            ],
            out_specs=pl.BlockSpec((block, head_size), lambda h, i, m: (i, h)),
        ),
        compiler_params=pltpu.CompilerParams(
            dimension_semantics=("arbitrary", "arbitrary"),
            vmem_limit_bytes=48 * 1024 * 1024,
        ),
    )(meta, q_rows, kv_all, kv_all)


def shards(
    queries, kv_pairs, residual, norm_gain, o_weight, w_in, w_down, expert_ids, route_weights
):
    tok_dev = queries.shape[0]
    width = residual.shape[1]
    n_sa = lax.axis_size("sa")
    n_sb = lax.axis_size("sb")
    n_seq = n_sa * n_sb
    n_grp = lax.axis_size("grp")
    devices = n_seq * n_grp
    head_size = HD
    heads_all = queries.shape[1] // head_size
    key_heads = kv_pairs.shape[2] // head_size
    sharing = heads_all // key_heads
    heads_here = heads_all // n_sa
    block_rows = o_weight.shape[0]
    assert sharing % heads_here == 0
    sa = lax.axis_index("sa")
    sb = lax.axis_index("sb")

    pair = lax.axis_index("grp") % 2
    half = o_weight.shape[1] // 2
    w_mine = lax.all_gather(
        lax.dynamic_slice_in_dim(o_weight, pair * half, half, axis=1), "sb", axis=0, tiled=True
    )
    q_send = queries.reshape(tok_dev, n_sa, heads_here * head_size).transpose(1, 0, 2)
    kv_heads = kv_pairs.reshape(2, tok_dev, key_heads, head_size)
    head_of_dest = (jnp.arange(n_sa) * heads_here) // sharing
    kv_send = jnp.take(kv_heads, head_of_dest, axis=2)
    kv_send = kv_send.transpose(2, 1, 0, 3).reshape(n_sa, tok_dev, 2 * head_size)
    packed = lax.all_to_all(
        jnp.concatenate([q_send, kv_send], axis=2), "sa", split_axis=0, concat_axis=0, tiled=True
    )
    q_rows = packed[:, :, : heads_here * head_size].reshape(n_sa * tok_dev, heads_here * head_size)
    kv_col = packed[:, :, heads_here * head_size :]
    kv_grid = lax.all_to_all(
        jnp.broadcast_to(kv_col[None], (n_sb,) + kv_col.shape), "sb", split_axis=0,
        concat_axis=0, tiled=True,
    )
    kv_all = kv_grid.transpose(1, 0, 2, 3).reshape(n_seq * tok_dev, 2 * head_size)
    meta = jnp.stack([sb, jnp.zeros_like(sb)]).astype(jnp.int32)
    attended = attention(meta, q_rows, kv_all, heads_here, head_size, tok_dev, n_sb)

    w_mine, attended = lax.optimization_barrier((w_mine, attended))
    w_other = lax.ppermute(w_mine, "grp", [(g, g ^ 1) for g in range(n_grp)])
    w_rows = jnp.zeros((w_mine.shape[0], 2 * half), o_weight.dtype)
    w_rows = lax.dynamic_update_slice_in_dim(w_rows, w_mine, pair * half, axis=1)
    w_rows = lax.dynamic_update_slice_in_dim(w_rows, w_other, (1 - pair) * half, axis=1)

    partial_sum = None
    for j in range(w_rows.shape[0] // block_rows):
        cols = slice(j * block_rows, (j + 1) * block_rows)
        partial_j = jnp.dot(
            attended[:, cols], w_rows[cols], preferred_element_type=jnp.float32
        ).astype(jnp.bfloat16).astype(jnp.float32)
        partial_sum = partial_j if partial_sum is None else partial_sum + partial_j
    attn_out = lax.psum_scatter(
        partial_sum.astype(jnp.bfloat16), "sa", scatter_dimension=0, tiled=True
    ).astype(jnp.float32)
    mixed = residual.astype(jnp.float32) + attn_out
    mean_square = jnp.mean(mixed * mixed, axis=1, keepdims=True)
    normed = (mixed * lax.rsqrt(mean_square + 1e-06) * norm_gain.astype(jnp.float32)).astype(
        jnp.bfloat16
    )

    top_count = expert_ids.shape[1]
    capacity = 2 * tok_dev * top_count // devices
    slots = devices * capacity
    flat_ids = expert_ids.reshape(-1)
    flat_weights = route_weights.reshape(-1)
    n_flat = flat_ids.shape[0]
    onehot = (flat_ids[:, None] == jnp.arange(devices, dtype=jnp.int32)[None, :]).astype(
        jnp.bfloat16
    )
    row = lax.broadcasted_iota(jnp.int32, (n_flat, n_flat), 0)
    col = lax.broadcasted_iota(jnp.int32, (n_flat, n_flat), 1)
    before = (col < row).astype(jnp.bfloat16)
    earlier = jnp.dot(before, onehot, preferred_element_type=jnp.float32)
    rank = jnp.sum(earlier * onehot.astype(jnp.float32), axis=1).astype(jnp.int32)
    halves = 2
    cap_half = capacity // halves
    slots_half = devices * cap_half
    slot_index = (rank // cap_half) * slots_half + flat_ids * cap_half + rank % cap_half
    picks = slot_index[:, None] == jnp.arange(slots, dtype=jnp.int32)[None, :]
    token_slots = jnp.any(picks.reshape(tok_dev, top_count, slots), axis=1).astype(jnp.bfloat16)
    ffe_width = w_down.shape[1]
    returned = []
    for h in range(halves):
        outgoing_rows = lax.dot_general(
            token_slots[:, h * slots_half : (h + 1) * slots_half], normed,
            (((0,), (0,)), ((), ())), preferred_element_type=jnp.float32,
        ).astype(jnp.bfloat16).reshape(devices, cap_half, width)
        arrived = lax.all_to_all(
            outgoing_rows, ("grp", "sa", "sb"), split_axis=0, concat_axis=0, tiled=True
        )
        flat_rows = arrived.reshape(-1, width)
        projected = jnp.dot(flat_rows, w_in[0], preferred_element_type=jnp.float32)
        hidden = (jax.nn.silu(projected[:, :ffe_width]) * projected[:, ffe_width:]).astype(
            jnp.bfloat16
        )
        produced = jnp.dot(hidden, w_down[0], preferred_element_type=jnp.float32).astype(
            jnp.bfloat16
        )
        returned.append(
            lax.all_to_all(
                produced.reshape(arrived.shape), ("grp", "sa", "sb"), split_axis=0,
                concat_axis=0, tiled=True,
            ).reshape(slots_half, width)
        )
    returned = jnp.concatenate(returned, axis=0)
    picks_by_choice = picks.reshape(tok_dev, top_count, slots).transpose(1, 0, 2)
    picked = jnp.dot(
        picks_by_choice.reshape(n_flat, slots).astype(jnp.bfloat16),
        returned,
        preferred_element_type=jnp.float32,
    ).reshape(top_count, tok_dev, width)
    weights_by_choice = route_weights.T.reshape(top_count, tok_dev, 1)
    combined = jnp.sum(picked * weights_by_choice, axis=0)
    return (mixed + combined).astype(jnp.bfloat16)


def solution(mesh):
    n_grp, n_seq = mesh.shape["grp"], mesh.shape["seq"]
    n_sb = math.isqrt(n_seq)
    grid = Mesh(mesh.devices.reshape(n_grp, n_seq // n_sb, n_sb), ("grp", "sa", "sb"))
    tokens = ("grp", "sa", "sb")
    return jax.shard_map(
        shards,
        mesh=grid,
        in_specs=(
            P(tokens, None),
            P(None, tokens, None),
            P(tokens, None),
            P(),
            P(("sa", "sb"), None),
            P(tokens, None, None),
            P(tokens, None, None),
            P(tokens, None),
            P(tokens, None),
        ),
        out_specs=P(tokens, None),
        check_vma=False,
    )
```

```python
import functools
import math

import jax
import jax.numpy as jnp
from jax import lax
from jax.experimental import pallas as pl
from jax.experimental.pallas import tpu as pltpu
from jax.sharding import Mesh, PartitionSpec as P

HD = 128
Q_BLOCK = 256


def _attend_kernel(meta_ref, q_ref, k_ref, v_ref, o_ref, *, block, scale, tok_dev, n_sb):
    qi = pl.program_id(1)
    sb = meta_ref[0]
    q = q_ref[...]
    k = k_ref[...]
    length = k.shape[0]
    scores = lax.dot_general(
        q, k, (((1,), (1,)), ((), ())), preferred_element_type=jnp.float32
    ) * scale
    local = qi * block + lax.broadcasted_iota(jnp.int32, (block, length), 0)
    q_pos = ((local // tok_dev) * n_sb + sb) * tok_dev + local % tok_dev
    k_pos = lax.broadcasted_iota(jnp.int32, (block, length), 1)
    scores = jnp.where(k_pos <= q_pos, scores, jnp.float32(-1e30))
    top = jnp.max(scores, axis=1, keepdims=True)
    weights = jnp.exp(scores - top)
    total = jnp.sum(weights, axis=1, keepdims=True)
    probs = (weights / total).astype(jnp.bfloat16)
    o_ref[...] = jnp.dot(probs, v_ref[...], preferred_element_type=jnp.float32).astype(
        o_ref.dtype
    )


def attention(meta, q_rows, kv_all, heads, head_size, tok_dev, n_sb):
    rows = q_rows.shape[0]
    seq_len = kv_all.shape[0]
    block = min(Q_BLOCK, rows)
    kernel = functools.partial(
        _attend_kernel, block=block, scale=1.0 / head_size**0.5, tok_dev=tok_dev, n_sb=n_sb
    )
    return pl.pallas_call(
        kernel,
        out_shape=jax.ShapeDtypeStruct((rows, heads * head_size), jnp.bfloat16),
        grid_spec=pltpu.PrefetchScalarGridSpec(
            num_scalar_prefetch=1,
            grid=(heads, rows // block),
            in_specs=[
                pl.BlockSpec((block, head_size), lambda h, i, m: (i, h)),
                pl.BlockSpec((seq_len, head_size), lambda h, i, m: (0, 0)),
                pl.BlockSpec((seq_len, head_size), lambda h, i, m: (0, 1)),
            ],
            out_specs=pl.BlockSpec((block, head_size), lambda h, i, m: (i, h)),
        ),
        compiler_params=pltpu.CompilerParams(
            dimension_semantics=("arbitrary", "arbitrary"),
            vmem_limit_bytes=48 * 1024 * 1024,
        ),
    )(meta, q_rows, kv_all, kv_all)


def shards(
    queries, kv_pairs, residual, norm_gain, o_weight, w_in, w_down, expert_ids, route_weights
):
    tok_dev = queries.shape[0]
    width = residual.shape[1]
    n_sa = lax.axis_size("sa")
    n_sb = lax.axis_size("sb")
    n_seq = n_sa * n_sb
    n_grp = lax.axis_size("grp")
    devices = n_seq * n_grp
    head_size = HD
    heads_all = queries.shape[1] // head_size
    key_heads = kv_pairs.shape[2] // head_size
    sharing = heads_all // key_heads
    heads_here = heads_all // n_sa
    block_rows = o_weight.shape[0]
    assert sharing % heads_here == 0
    sa = lax.axis_index("sa")
    sb = lax.axis_index("sb")

    pair = lax.axis_index("grp") % 2
    half = o_weight.shape[1] // 2
    w_mine = lax.all_gather(
        lax.dynamic_slice_in_dim(o_weight, pair * half, half, axis=1), "sb", axis=0, tiled=True
    )
    q_send = queries.reshape(tok_dev, n_sa, heads_here * head_size).transpose(1, 0, 2)
    kv_heads = kv_pairs.reshape(2, tok_dev, key_heads, head_size)
    head_of_dest = (jnp.arange(n_sa) * heads_here) // sharing
    kv_send = jnp.take(kv_heads, head_of_dest, axis=2)
    kv_send = kv_send.transpose(2, 1, 0, 3).reshape(n_sa, tok_dev, 2 * head_size)
    packed = lax.all_to_all(
        jnp.concatenate([q_send, kv_send], axis=2), "sa", split_axis=0, concat_axis=0, tiled=True
    )
    q_rows = packed[:, :, : heads_here * head_size].reshape(n_sa * tok_dev, heads_here * head_size)
    kv_col = packed[:, :, heads_here * head_size :]
    kv_grid = lax.all_to_all(
        jnp.broadcast_to(kv_col[None], (n_sb,) + kv_col.shape), "sb", split_axis=0,
        concat_axis=0, tiled=True,
    )
    kv_all = kv_grid.transpose(1, 0, 2, 3).reshape(n_seq * tok_dev, 2 * head_size)
    meta = jnp.stack([sb, jnp.zeros_like(sb)]).astype(jnp.int32)
    attended = attention(meta, q_rows, kv_all, heads_here, head_size, tok_dev, n_sb)

    w_mine, attended = lax.optimization_barrier((w_mine, attended))
    w_other = lax.ppermute(w_mine, "grp", [(g, g ^ 1) for g in range(n_grp)])
    w_rows = jnp.zeros((w_mine.shape[0], 2 * half), o_weight.dtype)
    w_rows = lax.dynamic_update_slice_in_dim(w_rows, w_mine, pair * half, axis=1)
    w_rows = lax.dynamic_update_slice_in_dim(w_rows, w_other, (1 - pair) * half, axis=1)

    partial_sum = None
    for j in range(w_rows.shape[0] // block_rows):
        cols = slice(j * block_rows, (j + 1) * block_rows)
        partial_j = jnp.dot(
            attended[:, cols], w_rows[cols], preferred_element_type=jnp.float32
        ).astype(jnp.bfloat16).astype(jnp.float32)
        partial_sum = partial_j if partial_sum is None else partial_sum + partial_j
    attn_out = lax.psum_scatter(
        partial_sum.astype(jnp.bfloat16), "sa", scatter_dimension=0, tiled=True
    ).astype(jnp.float32)
    mixed = residual.astype(jnp.float32) + attn_out
    mean_square = jnp.mean(mixed * mixed, axis=1, keepdims=True)
    normed = (mixed * lax.rsqrt(mean_square + 1e-06) * norm_gain.astype(jnp.float32)).astype(
        jnp.bfloat16
    )

    top_count = expert_ids.shape[1]
    capacity = 2 * tok_dev * top_count // devices
    slots = devices * capacity
    flat_ids = expert_ids.reshape(-1)
    flat_weights = route_weights.reshape(-1)
    n_flat = flat_ids.shape[0]
    onehot = (flat_ids[:, None] == jnp.arange(devices, dtype=jnp.int32)[None, :]).astype(
        jnp.bfloat16
    )
    row = lax.broadcasted_iota(jnp.int32, (n_flat, n_flat), 0)
    col = lax.broadcasted_iota(jnp.int32, (n_flat, n_flat), 1)
    before = (col < row).astype(jnp.bfloat16)
    earlier = jnp.dot(before, onehot, preferred_element_type=jnp.float32)
    rank = jnp.sum(earlier * onehot.astype(jnp.float32), axis=1).astype(jnp.int32)
    slot_index = flat_ids * capacity + rank
    picks = slot_index[:, None] == jnp.arange(slots, dtype=jnp.int32)[None, :]
    token_slots = jnp.any(picks.reshape(tok_dev, top_count, slots), axis=1).astype(jnp.bfloat16)
    ffe_width = w_down.shape[1]
    halves = 2
    part = width // halves
    projected = None
    for h in range(halves):
        outgoing_rows = lax.dot_general(
            token_slots, normed[:, h * part : (h + 1) * part], (((0,), (0,)), ((), ())),
            preferred_element_type=jnp.float32,
        ).astype(jnp.bfloat16).reshape(devices, capacity, part)
        arrived = lax.all_to_all(
            outgoing_rows, ("grp", "sa", "sb"), split_axis=0, concat_axis=0, tiled=True
        )
        term = jnp.dot(
            arrived.reshape(-1, part), w_in[0, h * part : (h + 1) * part],
            preferred_element_type=jnp.float32,
        )
        projected = term if projected is None else projected + term
    hidden = (jax.nn.silu(projected[:, :ffe_width]) * projected[:, ffe_width:]).astype(jnp.bfloat16)
    picks_by_choice = picks.reshape(tok_dev, top_count, slots).transpose(1, 0, 2)
    picks_by_choice = picks_by_choice.reshape(n_flat, slots).astype(jnp.bfloat16)
    weights_by_choice = route_weights.T.reshape(top_count, tok_dev, 1)
    combined = []
    for h in range(halves):
        produced = jnp.dot(
            hidden, w_down[0, :, h * part : (h + 1) * part], preferred_element_type=jnp.float32
        ).astype(jnp.bfloat16)
        returned = lax.all_to_all(
            produced.reshape(devices, capacity, part), ("grp", "sa", "sb"), split_axis=0,
            concat_axis=0, tiled=True,
        ).reshape(slots, part)
        picked = jnp.dot(
            picks_by_choice, returned, preferred_element_type=jnp.float32
        ).reshape(top_count, tok_dev, part)
        combined.append(jnp.sum(picked * weights_by_choice, axis=0))
    combined = jnp.concatenate(combined, axis=1)
    return (mixed + combined).astype(jnp.bfloat16)


def solution(mesh):
    n_grp, n_seq = mesh.shape["grp"], mesh.shape["seq"]
    n_sb = math.isqrt(n_seq)
    grid = Mesh(mesh.devices.reshape(n_grp, n_seq // n_sb, n_sb), ("grp", "sa", "sb"))
    tokens = ("grp", "sa", "sb")
    return jax.shard_map(
        shards,
        mesh=grid,
        in_specs=(
            P(tokens, None),
            P(None, tokens, None),
            P(tokens, None),
            P(),
            P(("sa", "sb"), None),
            P(tokens, None, None),
            P(tokens, None, None),
            P(tokens, None),
            P(tokens, None),
        ),
        out_specs=P(tokens, None),
        check_vma=False,
    )
```

```python
import functools
import math

import jax
import jax.numpy as jnp
from jax import lax
from jax.experimental import pallas as pl
from jax.experimental.pallas import tpu as pltpu
from jax.sharding import Mesh, PartitionSpec as P

HD = 128
Q_BLOCK = 256


def _attend_kernel(meta_ref, q_ref, k_ref, v_ref, o_ref, *, block, scale, tok_dev, n_sb):
    qi = pl.program_id(1)
    sb = meta_ref[0]

    def attend(length):
        q = q_ref[...]
        k = k_ref[:length, :]
        scores = lax.dot_general(
            q, k, (((1,), (1,)), ((), ())), preferred_element_type=jnp.float32
        ) * scale
        local = qi * block + lax.broadcasted_iota(jnp.int32, (block, length), 0)
        q_pos = ((local // tok_dev) * n_sb + sb) * tok_dev + local % tok_dev
        k_pos = lax.broadcasted_iota(jnp.int32, (block, length), 1)
        scores = jnp.where(k_pos <= q_pos, scores, jnp.float32(-1e30))
        top = jnp.max(scores, axis=1, keepdims=True)
        weights = jnp.exp(scores - top)
        total = jnp.sum(weights, axis=1, keepdims=True)
        probs = (weights / total).astype(jnp.bfloat16)
        o_ref[...] = jnp.dot(
            probs, v_ref[:length, :], preferred_element_type=jnp.float32
        ).astype(o_ref.dtype)

    seq_len = k_ref.shape[0]
    for i in range(seq_len):
        length = min(seq_len, (i + 1) * block * n_sb)
        if length == seq_len:
            pl.when(qi >= i)(lambda: attend(seq_len))
            break
        pl.when(qi == i)(functools.partial(attend, length))


def attention(meta, q_rows, kv_all, heads, head_size, tok_dev, n_sb):
    rows = q_rows.shape[0]
    seq_len = kv_all.shape[0]
    block = min(Q_BLOCK, rows)
    kernel = functools.partial(
        _attend_kernel, block=block, scale=1.0 / head_size**0.5, tok_dev=tok_dev, n_sb=n_sb
    )
    return pl.pallas_call(
        kernel,
        out_shape=jax.ShapeDtypeStruct((rows, heads * head_size), jnp.bfloat16),
        grid_spec=pltpu.PrefetchScalarGridSpec(
            num_scalar_prefetch=1,
            grid=(heads, rows // block),
            in_specs=[
                pl.BlockSpec((block, head_size), lambda h, i, m: (i, h)),
                pl.BlockSpec((seq_len, head_size), lambda h, i, m: (0, 0)),
                pl.BlockSpec((seq_len, head_size), lambda h, i, m: (0, 1)),
            ],
            out_specs=pl.BlockSpec((block, head_size), lambda h, i, m: (i, h)),
        ),
        compiler_params=pltpu.CompilerParams(
            dimension_semantics=("arbitrary", "arbitrary"),
            vmem_limit_bytes=48 * 1024 * 1024,
        ),
    )(meta, q_rows, kv_all, kv_all)


def shards(
    queries, kv_pairs, residual, norm_gain, o_weight, w_in, w_down, expert_ids, route_weights
):
    tok_dev = queries.shape[0]
    width = residual.shape[1]
    n_sa = lax.axis_size("sa")
    n_sb = lax.axis_size("sb")
    n_seq = n_sa * n_sb
    n_grp = lax.axis_size("grp")
    devices = n_seq * n_grp
    head_size = HD
    heads_all = queries.shape[1] // head_size
    key_heads = kv_pairs.shape[2] // head_size
    sharing = heads_all // key_heads
    heads_here = heads_all // n_sa
    block_rows = o_weight.shape[0]
    assert sharing % heads_here == 0
    sa = lax.axis_index("sa")
    sb = lax.axis_index("sb")

    pair = lax.axis_index("grp") % 2
    half = o_weight.shape[1] // 2
    w_mine = lax.all_gather(
        lax.dynamic_slice_in_dim(o_weight, pair * half, half, axis=1), "sb", axis=0, tiled=True
    )
    q_send = queries.reshape(tok_dev, n_sa, heads_here * head_size).transpose(1, 0, 2)
    kv_heads = kv_pairs.reshape(2, tok_dev, key_heads, head_size)
    head_of_dest = (jnp.arange(n_sa) * heads_here) // sharing
    kv_send = jnp.take(kv_heads, head_of_dest, axis=2)
    kv_send = kv_send.transpose(2, 1, 0, 3).reshape(n_sa, tok_dev, 2 * head_size)
    packed = lax.all_to_all(
        jnp.concatenate([q_send, kv_send], axis=2), "sa", split_axis=0, concat_axis=0, tiled=True
    )
    q_rows = packed[:, :, : heads_here * head_size].reshape(n_sa * tok_dev, heads_here * head_size)
    kv_col = packed[:, :, heads_here * head_size :]
    kv_grid = lax.all_to_all(
        jnp.broadcast_to(kv_col[None], (n_sb,) + kv_col.shape), "sb", split_axis=0,
        concat_axis=0, tiled=True,
    )
    kv_all = kv_grid.transpose(1, 0, 2, 3).reshape(n_seq * tok_dev, 2 * head_size)
    meta = jnp.stack([sb, jnp.zeros_like(sb)]).astype(jnp.int32)
    attended = attention(meta, q_rows, kv_all, heads_here, head_size, tok_dev, n_sb)

    w_mine, attended = lax.optimization_barrier((w_mine, attended))
    w_other = lax.ppermute(w_mine, "grp", [(g, g ^ 1) for g in range(n_grp)])
    w_rows = jnp.zeros((w_mine.shape[0], 2 * half), o_weight.dtype)
    w_rows = lax.dynamic_update_slice_in_dim(w_rows, w_mine, pair * half, axis=1)
    w_rows = lax.dynamic_update_slice_in_dim(w_rows, w_other, (1 - pair) * half, axis=1)

    partial_sum = None
    for j in range(w_rows.shape[0] // block_rows):
        cols = slice(j * block_rows, (j + 1) * block_rows)
        partial_j = jnp.dot(
            attended[:, cols], w_rows[cols], preferred_element_type=jnp.float32
        ).astype(jnp.bfloat16).astype(jnp.float32)
        partial_sum = partial_j if partial_sum is None else partial_sum + partial_j
    attn_out = lax.psum_scatter(
        partial_sum.astype(jnp.bfloat16), "sa", scatter_dimension=0, tiled=True
    ).astype(jnp.float32)
    mixed = residual.astype(jnp.float32) + attn_out
    mean_square = jnp.mean(mixed * mixed, axis=1, keepdims=True)
    normed = (mixed * lax.rsqrt(mean_square + 1e-06) * norm_gain.astype(jnp.float32)).astype(
        jnp.bfloat16
    )

    top_count = expert_ids.shape[1]
    capacity = 2 * tok_dev * top_count // devices
    slots = devices * capacity
    flat_ids = expert_ids.reshape(-1)
    flat_weights = route_weights.reshape(-1)
    n_flat = flat_ids.shape[0]
    onehot = (flat_ids[:, None] == jnp.arange(devices, dtype=jnp.int32)[None, :]).astype(
        jnp.bfloat16
    )
    row = lax.broadcasted_iota(jnp.int32, (n_flat, n_flat), 0)
    col = lax.broadcasted_iota(jnp.int32, (n_flat, n_flat), 1)
    before = (col < row).astype(jnp.bfloat16)
    earlier = jnp.dot(before, onehot, preferred_element_type=jnp.float32)
    rank = jnp.sum(earlier * onehot.astype(jnp.float32), axis=1).astype(jnp.int32)
    slot_index = flat_ids * capacity + rank
    picks = slot_index[:, None] == jnp.arange(slots, dtype=jnp.int32)[None, :]
    token_slots = jnp.any(picks.reshape(tok_dev, top_count, slots), axis=1).astype(jnp.bfloat16)
    outgoing_rows = lax.dot_general(
        token_slots, normed, (((0,), (0,)), ((), ())), preferred_element_type=jnp.float32
    ).astype(jnp.bfloat16)
    outgoing_rows = outgoing_rows.reshape(devices, capacity, width)
    ffe_width = w_down.shape[1]
    arrived = lax.all_to_all(outgoing_rows, ("grp", "sa", "sb"), split_axis=0, concat_axis=0, tiled=True)
    flat_rows = arrived.reshape(-1, width)
    projected = jnp.dot(flat_rows, w_in[0], preferred_element_type=jnp.float32)
    hidden = (jax.nn.silu(projected[:, :ffe_width]) * projected[:, ffe_width:]).astype(jnp.bfloat16)
    produced = jnp.dot(hidden, w_down[0], preferred_element_type=jnp.float32).astype(jnp.bfloat16)
    returned = lax.all_to_all(
        produced.reshape(arrived.shape), ("grp", "sa", "sb"), split_axis=0, concat_axis=0, tiled=True
    )
    returned = returned.reshape(slots, width)
    picks_by_choice = picks.reshape(tok_dev, top_count, slots).transpose(1, 0, 2)
    picked = jnp.dot(
        picks_by_choice.reshape(n_flat, slots).astype(jnp.bfloat16),
        returned,
        preferred_element_type=jnp.float32,
    ).reshape(top_count, tok_dev, width)
    weights_by_choice = route_weights.T.reshape(top_count, tok_dev, 1)
    combined = jnp.sum(picked * weights_by_choice, axis=0)
    return (mixed + combined).astype(jnp.bfloat16)


def solution(mesh):
    n_grp, n_seq = mesh.shape["grp"], mesh.shape["seq"]
    n_sb = math.isqrt(n_seq)
    grid = Mesh(mesh.devices.reshape(n_grp, n_seq // n_sb, n_sb), ("grp", "sa", "sb"))
    tokens = ("grp", "sa", "sb")
    return jax.shard_map(
        shards,
        mesh=grid,
        in_specs=(
            P(tokens, None),
            P(None, tokens, None),
            P(tokens, None),
            P(),
            P(("sa", "sb"), None),
            P(tokens, None, None),
            P(tokens, None, None),
            P(tokens, None),
            P(tokens, None),
        ),
        out_specs=P(tokens, None),
        check_vma=False,
    )
```

```python
import functools
import math

import jax
import jax.numpy as jnp
from jax import lax
from jax.experimental import pallas as pl
from jax.experimental.pallas import tpu as pltpu
from jax.sharding import Mesh, PartitionSpec as P

HD = 128
Q_BLOCK = 256


def _attend_kernel(meta_ref, q_ref, k_ref, v_ref, o_ref, *, block, scale, tok_dev, n_sb):
    qi = pl.program_id(1)
    sb = meta_ref[0]

    def attend(length):
        q = q_ref[...]
        k = k_ref[:length, :]
        scores = lax.dot_general(
            q, k, (((1,), (1,)), ((), ())), preferred_element_type=jnp.float32
        ) * scale
        local = qi * block + lax.broadcasted_iota(jnp.int32, (block, length), 0)
        q_pos = ((local // tok_dev) * n_sb + sb) * tok_dev + local % tok_dev
        k_pos = lax.broadcasted_iota(jnp.int32, (block, length), 1)
        scores = jnp.where(k_pos <= q_pos, scores, jnp.float32(-1e30))
        top = jnp.max(scores, axis=1, keepdims=True)
        weights = jnp.exp(scores - top)
        total = jnp.sum(weights, axis=1, keepdims=True)
        probs = (weights / total).astype(jnp.bfloat16)
        o_ref[...] = jnp.dot(
            probs, v_ref[:length, :], preferred_element_type=jnp.float32
        ).astype(o_ref.dtype)

    seq_len = k_ref.shape[0]
    for i in range(seq_len):
        length = min(seq_len, (i + 1) * block * n_sb)
        if length == seq_len:
            pl.when(qi >= i)(lambda: attend(seq_len))
            break
        pl.when(qi == i)(functools.partial(attend, length))


def attention(meta, q_rows, kv_all, heads, head_size, tok_dev, n_sb):
    rows = q_rows.shape[0]
    seq_len = kv_all.shape[0]
    block = min(Q_BLOCK, rows)
    kernel = functools.partial(
        _attend_kernel, block=block, scale=1.0 / head_size**0.5, tok_dev=tok_dev, n_sb=n_sb
    )
    return pl.pallas_call(
        kernel,
        out_shape=jax.ShapeDtypeStruct((rows, heads * head_size), jnp.bfloat16),
        grid_spec=pltpu.PrefetchScalarGridSpec(
            num_scalar_prefetch=1,
            grid=(heads, rows // block),
            in_specs=[
                pl.BlockSpec((block, head_size), lambda h, i, m: (i, h)),
                pl.BlockSpec((seq_len, head_size), lambda h, i, m: (0, 0)),
                pl.BlockSpec((seq_len, head_size), lambda h, i, m: (0, 1)),
            ],
            out_specs=pl.BlockSpec((block, head_size), lambda h, i, m: (i, h)),
        ),
        compiler_params=pltpu.CompilerParams(
            dimension_semantics=("arbitrary", "arbitrary"),
            vmem_limit_bytes=48 * 1024 * 1024,
        ),
    )(meta, q_rows, kv_all, kv_all)


def shards(
    queries, kv_pairs, residual, norm_gain, o_weight, w_in, w_down, expert_ids, route_weights
):
    tok_dev = queries.shape[0]
    width = residual.shape[1]
    n_sa = lax.axis_size("sa")
    n_sb = lax.axis_size("sb")
    n_seq = n_sa * n_sb
    n_grp = lax.axis_size("grp")
    devices = n_seq * n_grp
    head_size = HD
    heads_all = queries.shape[1] // head_size
    key_heads = kv_pairs.shape[2] // head_size
    sharing = heads_all // key_heads
    heads_here = heads_all // n_sa
    block_rows = o_weight.shape[0]
    assert sharing % heads_here == 0
    sa = lax.axis_index("sa")
    sb = lax.axis_index("sb")

    pair = lax.axis_index("grp") % 2
    half = o_weight.shape[1] // 2
    w_mine = lax.all_gather(
        lax.dynamic_slice_in_dim(o_weight, pair * half, half, axis=1), "sb", axis=0, tiled=True
    )
    q_send = queries.reshape(tok_dev, n_sa, heads_here * head_size).transpose(1, 0, 2)
    kv_heads = kv_pairs.reshape(2, tok_dev, key_heads, head_size)
    head_of_dest = (jnp.arange(n_sa) * heads_here) // sharing
    kv_send = jnp.take(kv_heads, head_of_dest, axis=2)
    kv_send = kv_send.transpose(2, 1, 0, 3).reshape(n_sa, tok_dev, 2 * head_size)
    packed = lax.all_to_all(
        jnp.concatenate([q_send, kv_send], axis=2), "sa", split_axis=0, concat_axis=0, tiled=True
    )
    q_rows = packed[:, :, : heads_here * head_size].reshape(n_sa * tok_dev, heads_here * head_size)
    kv_col = packed[:, :, heads_here * head_size :]
    kv_grid = lax.all_to_all(
        jnp.broadcast_to(kv_col[None], (n_sb,) + kv_col.shape), "sb", split_axis=0,
        concat_axis=0, tiled=True,
    )
    kv_all = kv_grid.transpose(1, 0, 2, 3).reshape(n_seq * tok_dev, 2 * head_size)
    meta = jnp.stack([sb, jnp.zeros_like(sb)]).astype(jnp.int32)
    attended = attention(meta, q_rows, kv_all, heads_here, head_size, tok_dev, n_sb)

    w_mine, attended = lax.optimization_barrier((w_mine, attended))
    w_other = lax.ppermute(w_mine, "grp", [(g, g ^ 1) for g in range(n_grp)])
    w_rows = jnp.concatenate([w_mine, w_other], axis=1)

    partial_sum = None
    for j in range(w_rows.shape[0] // block_rows):
        cols = slice(j * block_rows, (j + 1) * block_rows)
        partial_j = jnp.dot(
            attended[:, cols], w_rows[cols], preferred_element_type=jnp.float32
        ).astype(jnp.bfloat16).astype(jnp.float32)
        partial_sum = partial_j if partial_sum is None else partial_sum + partial_j
    swapped = lax.psum_scatter(
        partial_sum.astype(jnp.bfloat16), "sa", scatter_dimension=0, tiled=True
    )
    attn_out = lax.dynamic_slice_in_dim(
        jnp.concatenate([swapped, swapped], axis=1), pair * half, 2 * half, axis=1
    ).astype(jnp.float32)
    mixed = residual.astype(jnp.float32) + attn_out
    mean_square = jnp.mean(mixed * mixed, axis=1, keepdims=True)
    normed = (mixed * lax.rsqrt(mean_square + 1e-06) * norm_gain.astype(jnp.float32)).astype(
        jnp.bfloat16
    )

    top_count = expert_ids.shape[1]
    capacity = 2 * tok_dev * top_count // devices
    slots = devices * capacity
    flat_ids = expert_ids.reshape(-1)
    flat_weights = route_weights.reshape(-1)
    n_flat = flat_ids.shape[0]
    onehot = (flat_ids[:, None] == jnp.arange(devices, dtype=jnp.int32)[None, :]).astype(
        jnp.bfloat16
    )
    row = lax.broadcasted_iota(jnp.int32, (n_flat, n_flat), 0)
    col = lax.broadcasted_iota(jnp.int32, (n_flat, n_flat), 1)
    before = (col < row).astype(jnp.bfloat16)
    earlier = jnp.dot(before, onehot, preferred_element_type=jnp.float32)
    rank = jnp.sum(earlier * onehot.astype(jnp.float32), axis=1).astype(jnp.int32)
    slot_index = flat_ids * capacity + rank
    picks = slot_index[:, None] == jnp.arange(slots, dtype=jnp.int32)[None, :]
    token_slots = jnp.any(picks.reshape(tok_dev, top_count, slots), axis=1).astype(jnp.bfloat16)
    outgoing_rows = lax.dot_general(
        token_slots, normed, (((0,), (0,)), ((), ())), preferred_element_type=jnp.float32
    ).astype(jnp.bfloat16)
    outgoing_rows = outgoing_rows.reshape(devices, capacity, width)
    ffe_width = w_down.shape[1]
    arrived = lax.all_to_all(outgoing_rows, ("grp", "sa", "sb"), split_axis=0, concat_axis=0, tiled=True)
    flat_rows = arrived.reshape(-1, width)
    projected = jnp.dot(flat_rows, w_in[0], preferred_element_type=jnp.float32)
    hidden = (jax.nn.silu(projected[:, :ffe_width]) * projected[:, ffe_width:]).astype(jnp.bfloat16)
    produced = jnp.dot(hidden, w_down[0], preferred_element_type=jnp.float32).astype(jnp.bfloat16)
    returned = lax.all_to_all(
        produced.reshape(arrived.shape), ("grp", "sa", "sb"), split_axis=0, concat_axis=0, tiled=True
    )
    returned = returned.reshape(slots, width)
    picks_by_choice = picks.reshape(tok_dev, top_count, slots).transpose(1, 0, 2)
    picked = jnp.dot(
        picks_by_choice.reshape(n_flat, slots).astype(jnp.bfloat16),
        returned,
        preferred_element_type=jnp.float32,
    ).reshape(top_count, tok_dev, width)
    weights_by_choice = route_weights.T.reshape(top_count, tok_dev, 1)
    combined = jnp.sum(picked * weights_by_choice, axis=0)
    return (mixed + combined).astype(jnp.bfloat16)


def solution(mesh):
    n_grp, n_seq = mesh.shape["grp"], mesh.shape["seq"]
    n_sb = math.isqrt(n_seq)
    grid = Mesh(mesh.devices.reshape(n_grp, n_seq // n_sb, n_sb), ("grp", "sa", "sb"))
    tokens = ("grp", "sa", "sb")
    return jax.shard_map(
        shards,
        mesh=grid,
        in_specs=(
            P(tokens, None),
            P(None, tokens, None),
            P(tokens, None),
            P(),
            P(("sa", "sb"), None),
            P(tokens, None, None),
            P(tokens, None, None),
            P(tokens, None),
            P(tokens, None),
        ),
        out_specs=P(tokens, None),
        check_vma=False,
    )
```

```python
import functools
import math

import jax
import jax.numpy as jnp
from jax import lax
from jax.experimental import pallas as pl
from jax.experimental.pallas import tpu as pltpu
from jax.sharding import Mesh, PartitionSpec as P

HD = 128
Q_BLOCK = 256


def _attend_kernel(meta_ref, q_ref, k_ref, v_ref, o_ref, *, block, scale, tok_dev, n_sb):
    qi = pl.program_id(1)
    sb = meta_ref[0]

    def attend(length):
        q = q_ref[...]
        k = k_ref[:length, :]
        scores = lax.dot_general(
            q, k, (((1,), (1,)), ((), ())), preferred_element_type=jnp.float32
        ) * scale
        local = qi * block + lax.broadcasted_iota(jnp.int32, (block, length), 0)
        q_pos = ((local // tok_dev) * n_sb + sb) * tok_dev + local % tok_dev
        k_pos = lax.broadcasted_iota(jnp.int32, (block, length), 1)
        scores = jnp.where(k_pos <= q_pos, scores, jnp.float32(-1e30))
        top = jnp.max(scores, axis=1, keepdims=True)
        weights = jnp.exp(scores - top)
        total = jnp.sum(weights, axis=1, keepdims=True)
        probs = (weights / total).astype(jnp.bfloat16)
        o_ref[...] = jnp.dot(
            probs, v_ref[:length, :], preferred_element_type=jnp.float32
        ).astype(o_ref.dtype)

    seq_len = k_ref.shape[0]
    for i in range(seq_len):
        length = min(seq_len, (i + 1) * block * n_sb)
        if length == seq_len:
            pl.when(qi >= i)(lambda: attend(seq_len))
            break
        pl.when(qi == i)(functools.partial(attend, length))


def attention(meta, q_rows, kv_all, heads, head_size, tok_dev, n_sb):
    rows = q_rows.shape[0]
    seq_len = kv_all.shape[0]
    block = min(Q_BLOCK, rows)
    kernel = functools.partial(
        _attend_kernel, block=block, scale=1.0 / head_size**0.5, tok_dev=tok_dev, n_sb=n_sb
    )
    return pl.pallas_call(
        kernel,
        out_shape=jax.ShapeDtypeStruct((rows, heads * head_size), jnp.bfloat16),
        grid_spec=pltpu.PrefetchScalarGridSpec(
            num_scalar_prefetch=1,
            grid=(heads, rows // block),
            in_specs=[
                pl.BlockSpec((block, head_size), lambda h, i, m: (i, h)),
                pl.BlockSpec((seq_len, head_size), lambda h, i, m: (0, 0)),
                pl.BlockSpec((seq_len, head_size), lambda h, i, m: (0, 1)),
            ],
            out_specs=pl.BlockSpec((block, head_size), lambda h, i, m: (i, h)),
        ),
        compiler_params=pltpu.CompilerParams(
            dimension_semantics=("arbitrary", "arbitrary"),
            vmem_limit_bytes=48 * 1024 * 1024,
        ),
    )(meta, q_rows, kv_all, kv_all)


def shards(
    queries, kv_pairs, residual, norm_gain, o_weight, w_in, w_down, expert_ids, route_weights
):
    tok_dev = queries.shape[0]
    width = residual.shape[1]
    n_sa = lax.axis_size("sa")
    n_sb = lax.axis_size("sb")
    n_seq = n_sa * n_sb
    n_grp = lax.axis_size("grp")
    devices = n_seq * n_grp
    head_size = HD
    heads_all = queries.shape[1] // head_size
    key_heads = kv_pairs.shape[2] // head_size
    sharing = heads_all // key_heads
    heads_here = heads_all // n_sa
    block_rows = o_weight.shape[0]
    assert sharing % heads_here == 0
    sa = lax.axis_index("sa")
    sb = lax.axis_index("sb")

    pair = lax.axis_index("grp") % 2
    half = o_weight.shape[1] // 2
    w_mine = lax.all_gather(
        lax.dynamic_slice_in_dim(o_weight, pair * half, half, axis=1), "sb", axis=0, tiled=True
    )
    q_send = queries.reshape(tok_dev, n_sa, heads_here * head_size).transpose(1, 0, 2)
    kv_heads = kv_pairs.reshape(2, tok_dev, key_heads, head_size)
    head_of_dest = (jnp.arange(n_sa) * heads_here) // sharing
    kv_send = jnp.take(kv_heads, head_of_dest, axis=2)
    kv_send = kv_send.transpose(2, 1, 0, 3).reshape(n_sa, tok_dev, 2 * head_size)
    packed = lax.all_to_all(
        jnp.concatenate([q_send, kv_send], axis=2), "sa", split_axis=0, concat_axis=0, tiled=True
    )
    q_rows = packed[:, :, : heads_here * head_size].reshape(n_sa * tok_dev, heads_here * head_size)
    kv_col = packed[:, :, heads_here * head_size :]
    kv_grid = lax.all_to_all(
        jnp.broadcast_to(kv_col[None], (n_sb,) + kv_col.shape), "sb", split_axis=0,
        concat_axis=0, tiled=True,
    )
    kv_all = kv_grid.transpose(1, 0, 2, 3).reshape(n_seq * tok_dev, 2 * head_size)
    meta = jnp.stack([sb, jnp.zeros_like(sb)]).astype(jnp.int32)
    w_mine, kv_all = lax.optimization_barrier((w_mine, kv_all))
    w_other = lax.ppermute(w_mine, "grp", [(g, g ^ 1) for g in range(n_grp)])
    attended = attention(meta, q_rows, kv_all, heads_here, head_size, tok_dev, n_sb)
    w_rows = jnp.concatenate([w_mine, w_other], axis=1)

    partial_sum = None
    for j in range(w_rows.shape[0] // block_rows):
        cols = slice(j * block_rows, (j + 1) * block_rows)
        partial_j = jnp.dot(
            attended[:, cols], w_rows[cols], preferred_element_type=jnp.float32
        ).astype(jnp.bfloat16).astype(jnp.float32)
        partial_sum = partial_j if partial_sum is None else partial_sum + partial_j
    swapped = lax.psum_scatter(
        partial_sum.astype(jnp.bfloat16), "sa", scatter_dimension=0, tiled=True
    )
    attn_out = lax.dynamic_slice_in_dim(
        jnp.concatenate([swapped, swapped], axis=1), pair * half, 2 * half, axis=1
    ).astype(jnp.float32)
    mixed = residual.astype(jnp.float32) + attn_out
    mean_square = jnp.mean(mixed * mixed, axis=1, keepdims=True)
    normed = (mixed * lax.rsqrt(mean_square + 1e-06) * norm_gain.astype(jnp.float32)).astype(
        jnp.bfloat16
    )

    top_count = expert_ids.shape[1]
    capacity = 2 * tok_dev * top_count // devices
    slots = devices * capacity
    flat_ids = expert_ids.reshape(-1)
    flat_weights = route_weights.reshape(-1)
    n_flat = flat_ids.shape[0]
    onehot = (flat_ids[:, None] == jnp.arange(devices, dtype=jnp.int32)[None, :]).astype(
        jnp.bfloat16
    )
    row = lax.broadcasted_iota(jnp.int32, (n_flat, n_flat), 0)
    col = lax.broadcasted_iota(jnp.int32, (n_flat, n_flat), 1)
    before = (col < row).astype(jnp.bfloat16)
    earlier = jnp.dot(before, onehot, preferred_element_type=jnp.float32)
    rank = jnp.sum(earlier * onehot.astype(jnp.float32), axis=1).astype(jnp.int32)
    slot_index = flat_ids * capacity + rank
    picks = slot_index[:, None] == jnp.arange(slots, dtype=jnp.int32)[None, :]
    token_slots = jnp.any(picks.reshape(tok_dev, top_count, slots), axis=1).astype(jnp.bfloat16)
    outgoing_rows = lax.dot_general(
        token_slots, normed, (((0,), (0,)), ((), ())), preferred_element_type=jnp.float32
    ).astype(jnp.bfloat16)
    outgoing_rows = outgoing_rows.reshape(devices, capacity, width)
    ffe_width = w_down.shape[1]
    arrived = lax.all_to_all(outgoing_rows, ("grp", "sa", "sb"), split_axis=0, concat_axis=0, tiled=True)
    flat_rows = arrived.reshape(-1, width)
    projected = jnp.dot(flat_rows, w_in[0], preferred_element_type=jnp.float32)
    hidden = (jax.nn.silu(projected[:, :ffe_width]) * projected[:, ffe_width:]).astype(jnp.bfloat16)
    produced = jnp.dot(hidden, w_down[0], preferred_element_type=jnp.float32).astype(jnp.bfloat16)
    returned = lax.all_to_all(
        produced.reshape(arrived.shape), ("grp", "sa", "sb"), split_axis=0, concat_axis=0, tiled=True
    )
    returned = returned.reshape(slots, width)
    picks_by_choice = picks.reshape(tok_dev, top_count, slots).transpose(1, 0, 2)
    picked = jnp.dot(
        picks_by_choice.reshape(n_flat, slots).astype(jnp.bfloat16),
        returned,
        preferred_element_type=jnp.float32,
    ).reshape(top_count, tok_dev, width)
    weights_by_choice = route_weights.T.reshape(top_count, tok_dev, 1)
    combined = jnp.sum(picked * weights_by_choice, axis=0)
    return (mixed + combined).astype(jnp.bfloat16)


def solution(mesh):
    n_grp, n_seq = mesh.shape["grp"], mesh.shape["seq"]
    n_sb = math.isqrt(n_seq)
    grid = Mesh(mesh.devices.reshape(n_grp, n_seq // n_sb, n_sb), ("grp", "sa", "sb"))
    tokens = ("grp", "sa", "sb")
    return jax.shard_map(
        shards,
        mesh=grid,
        in_specs=(
            P(tokens, None),
            P(None, tokens, None),
            P(tokens, None),
            P(),
            P(("sa", "sb"), None),
            P(tokens, None, None),
            P(tokens, None, None),
            P(tokens, None),
            P(tokens, None),
        ),
        out_specs=P(tokens, None),
        check_vma=False,
    )
```

```python
import functools
import math

import jax
import jax.numpy as jnp
from jax import lax
from jax.experimental import pallas as pl
from jax.experimental.pallas import tpu as pltpu
from jax.sharding import Mesh, PartitionSpec as P

HD = 128
Q_BLOCK = 128


def _attend_kernel(meta_ref, q_ref, k_ref, v_ref, o_ref, *, block, scale, tok_dev, n_sb):
    qi = pl.program_id(1)
    sb = meta_ref[0]

    def attend(length):
        q = q_ref[...]
        k = k_ref[:length, :]
        scores = lax.dot_general(
            q, k, (((1,), (1,)), ((), ())), preferred_element_type=jnp.float32
        ) * scale
        local = qi * block + lax.broadcasted_iota(jnp.int32, (block, length), 0)
        q_pos = ((local // tok_dev) * n_sb + sb) * tok_dev + local % tok_dev
        k_pos = lax.broadcasted_iota(jnp.int32, (block, length), 1)
        scores = jnp.where(k_pos <= q_pos, scores, jnp.float32(-1e30))
        top = jnp.max(scores, axis=1, keepdims=True)
        weights = jnp.exp(scores - top)
        total = jnp.sum(weights, axis=1, keepdims=True)
        probs = (weights / total).astype(jnp.bfloat16)
        o_ref[...] = jnp.dot(
            probs, v_ref[:length, :], preferred_element_type=jnp.float32
        ).astype(o_ref.dtype)

    seq_len = k_ref.shape[0]
    for i in range(seq_len):
        length = min(seq_len, (i + 1) * block * n_sb)
        if length == seq_len:
            pl.when(qi >= i)(lambda: attend(seq_len))
            break
        pl.when(qi == i)(functools.partial(attend, length))


def attention(meta, q_rows, kv_all, heads, head_size, tok_dev, n_sb):
    rows = q_rows.shape[0]
    seq_len = kv_all.shape[0]
    block = min(Q_BLOCK, rows)
    kernel = functools.partial(
        _attend_kernel, block=block, scale=1.0 / head_size**0.5, tok_dev=tok_dev, n_sb=n_sb
    )
    return pl.pallas_call(
        kernel,
        out_shape=jax.ShapeDtypeStruct((rows, heads * head_size), jnp.bfloat16),
        grid_spec=pltpu.PrefetchScalarGridSpec(
            num_scalar_prefetch=1,
            grid=(heads, rows // block),
            in_specs=[
                pl.BlockSpec((block, head_size), lambda h, i, m: (i, h)),
                pl.BlockSpec((seq_len, head_size), lambda h, i, m: (0, 0)),
                pl.BlockSpec((seq_len, head_size), lambda h, i, m: (0, 1)),
            ],
            out_specs=pl.BlockSpec((block, head_size), lambda h, i, m: (i, h)),
        ),
        compiler_params=pltpu.CompilerParams(
            dimension_semantics=("arbitrary", "arbitrary"),
            vmem_limit_bytes=48 * 1024 * 1024,
        ),
    )(meta, q_rows, kv_all, kv_all)


def shards(
    queries, kv_pairs, residual, norm_gain, o_weight, w_in, w_down, expert_ids, route_weights
):
    tok_dev = queries.shape[0]
    width = residual.shape[1]
    n_sa = lax.axis_size("sa")
    n_sb = lax.axis_size("sb")
    n_seq = n_sa * n_sb
    n_grp = lax.axis_size("grp")
    devices = n_seq * n_grp
    head_size = HD
    heads_all = queries.shape[1] // head_size
    key_heads = kv_pairs.shape[2] // head_size
    sharing = heads_all // key_heads
    heads_here = heads_all // n_sa
    block_rows = o_weight.shape[0]
    assert sharing % heads_here == 0
    sa = lax.axis_index("sa")
    sb = lax.axis_index("sb")

    pair = lax.axis_index("grp") % 2
    half = o_weight.shape[1] // 2
    w_mine = lax.all_gather(
        lax.dynamic_slice_in_dim(o_weight, pair * half, half, axis=1), "sb", axis=0, tiled=True
    )
    q_send = queries.reshape(tok_dev, n_sa, heads_here * head_size).transpose(1, 0, 2)
    kv_heads = kv_pairs.reshape(2, tok_dev, key_heads, head_size)
    head_of_dest = (jnp.arange(n_sa) * heads_here) // sharing
    kv_send = jnp.take(kv_heads, head_of_dest, axis=2)
    kv_send = kv_send.transpose(2, 1, 0, 3).reshape(n_sa, tok_dev, 2 * head_size)
    packed = lax.all_to_all(
        jnp.concatenate([q_send, kv_send], axis=2), "sa", split_axis=0, concat_axis=0, tiled=True
    )
    q_rows = packed[:, :, : heads_here * head_size].reshape(n_sa * tok_dev, heads_here * head_size)
    kv_col = packed[:, :, heads_here * head_size :]
    kv_grid = lax.all_to_all(
        jnp.broadcast_to(kv_col[None], (n_sb,) + kv_col.shape), "sb", split_axis=0,
        concat_axis=0, tiled=True,
    )
    kv_all = kv_grid.transpose(1, 0, 2, 3).reshape(n_seq * tok_dev, 2 * head_size)
    meta = jnp.stack([sb, jnp.zeros_like(sb)]).astype(jnp.int32)
    attended = attention(meta, q_rows, kv_all, heads_here, head_size, tok_dev, n_sb)

    w_mine, attended = lax.optimization_barrier((w_mine, attended))
    w_other = lax.ppermute(w_mine, "grp", [(g, g ^ 1) for g in range(n_grp)])
    w_rows = jnp.concatenate([w_mine, w_other], axis=1)

    partial_sum = None
    for j in range(w_rows.shape[0] // block_rows):
        cols = slice(j * block_rows, (j + 1) * block_rows)
        partial_j = jnp.dot(
            attended[:, cols], w_rows[cols], preferred_element_type=jnp.float32
        ).astype(jnp.bfloat16).astype(jnp.float32)
        partial_sum = partial_j if partial_sum is None else partial_sum + partial_j
    swapped = lax.psum_scatter(
        partial_sum.astype(jnp.bfloat16), "sa", scatter_dimension=0, tiled=True
    )
    attn_out = lax.dynamic_slice_in_dim(
        jnp.concatenate([swapped, swapped], axis=1), pair * half, 2 * half, axis=1
    ).astype(jnp.float32)
    mixed = residual.astype(jnp.float32) + attn_out
    mean_square = jnp.mean(mixed * mixed, axis=1, keepdims=True)
    normed = (mixed * lax.rsqrt(mean_square + 1e-06) * norm_gain.astype(jnp.float32)).astype(
        jnp.bfloat16
    )

    top_count = expert_ids.shape[1]
    capacity = 2 * tok_dev * top_count // devices
    slots = devices * capacity
    flat_ids = expert_ids.reshape(-1)
    flat_weights = route_weights.reshape(-1)
    n_flat = flat_ids.shape[0]
    onehot = (flat_ids[:, None] == jnp.arange(devices, dtype=jnp.int32)[None, :]).astype(
        jnp.bfloat16
    )
    row = lax.broadcasted_iota(jnp.int32, (n_flat, n_flat), 0)
    col = lax.broadcasted_iota(jnp.int32, (n_flat, n_flat), 1)
    before = (col < row).astype(jnp.bfloat16)
    earlier = jnp.dot(before, onehot, preferred_element_type=jnp.float32)
    rank = jnp.sum(earlier * onehot.astype(jnp.float32), axis=1).astype(jnp.int32)
    slot_index = flat_ids * capacity + rank
    picks = slot_index[:, None] == jnp.arange(slots, dtype=jnp.int32)[None, :]
    token_slots = jnp.any(picks.reshape(tok_dev, top_count, slots), axis=1).astype(jnp.bfloat16)
    outgoing_rows = lax.dot_general(
        token_slots, normed, (((0,), (0,)), ((), ())), preferred_element_type=jnp.float32
    ).astype(jnp.bfloat16)
    outgoing_rows = outgoing_rows.reshape(devices, capacity, width)
    ffe_width = w_down.shape[1]
    arrived = lax.all_to_all(outgoing_rows, ("grp", "sa", "sb"), split_axis=0, concat_axis=0, tiled=True)
    flat_rows = arrived.reshape(-1, width)
    projected = jnp.dot(flat_rows, w_in[0], preferred_element_type=jnp.float32)
    hidden = (jax.nn.silu(projected[:, :ffe_width]) * projected[:, ffe_width:]).astype(jnp.bfloat16)
    produced = jnp.dot(hidden, w_down[0], preferred_element_type=jnp.float32).astype(jnp.bfloat16)
    returned = lax.all_to_all(
        produced.reshape(arrived.shape), ("grp", "sa", "sb"), split_axis=0, concat_axis=0, tiled=True
    )
    returned = returned.reshape(slots, width)
    picks_by_choice = picks.reshape(tok_dev, top_count, slots).transpose(1, 0, 2)
    picked = jnp.dot(
        picks_by_choice.reshape(n_flat, slots).astype(jnp.bfloat16),
        returned,
        preferred_element_type=jnp.float32,
    ).reshape(top_count, tok_dev, width)
    weights_by_choice = route_weights.T.reshape(top_count, tok_dev, 1)
    combined = jnp.sum(picked * weights_by_choice, axis=0)
    return (mixed + combined).astype(jnp.bfloat16)


def solution(mesh):
    n_grp, n_seq = mesh.shape["grp"], mesh.shape["seq"]
    n_sb = math.isqrt(n_seq)
    grid = Mesh(mesh.devices.reshape(n_grp, n_seq // n_sb, n_sb), ("grp", "sa", "sb"))
    tokens = ("grp", "sa", "sb")
    return jax.shard_map(
        shards,
        mesh=grid,
        in_specs=(
            P(tokens, None),
            P(None, tokens, None),
            P(tokens, None),
            P(),
            P(("sa", "sb"), None),
            P(tokens, None, None),
            P(tokens, None, None),
            P(tokens, None),
            P(tokens, None),
        ),
        out_specs=P(tokens, None),
        check_vma=False,
    )
```

```python
import functools
import math

import jax
import jax.numpy as jnp
from jax import lax
from jax.experimental import pallas as pl
from jax.experimental.pallas import tpu as pltpu
from jax.sharding import Mesh, PartitionSpec as P

HD = 128
Q_BLOCK = 256


def _attend_kernel(meta_ref, q_ref, k_ref, v_ref, o_ref, *, block, scale, tok_dev, n_sb):
    qi = pl.program_id(1)
    sb = meta_ref[0]

    def attend(length):
        q = q_ref[...]
        k = k_ref[:length, :]
        scores = lax.dot_general(
            q, k, (((1,), (1,)), ((), ())), preferred_element_type=jnp.float32
        ) * scale
        local = qi * block + lax.broadcasted_iota(jnp.int32, (block, length), 0)
        q_pos = ((local // tok_dev) * n_sb + sb) * tok_dev + local % tok_dev
        k_pos = lax.broadcasted_iota(jnp.int32, (block, length), 1)
        scores = jnp.where(k_pos <= q_pos, scores, jnp.float32(-1e30))
        top = jnp.max(scores, axis=1, keepdims=True)
        weights = jnp.exp(scores - top)
        total = jnp.sum(weights, axis=1, keepdims=True)
        probs = (weights / total).astype(jnp.bfloat16)
        o_ref[...] = jnp.dot(
            probs, v_ref[:length, :], preferred_element_type=jnp.float32
        ).astype(o_ref.dtype)

    seq_len = k_ref.shape[0]
    for i in range(seq_len):
        length = min(seq_len, (i + 1) * block * n_sb)
        if length == seq_len:
            pl.when(qi >= i)(lambda: attend(seq_len))
            break
        pl.when(qi == i)(functools.partial(attend, length))


def attention(meta, q_rows, kv_all, heads, head_size, tok_dev, n_sb):
    rows = q_rows.shape[0]
    seq_len = kv_all.shape[0]
    block = min(Q_BLOCK, rows)
    kernel = functools.partial(
        _attend_kernel, block=block, scale=1.0 / head_size**0.5, tok_dev=tok_dev, n_sb=n_sb
    )
    return pl.pallas_call(
        kernel,
        out_shape=jax.ShapeDtypeStruct((rows, heads * head_size), jnp.bfloat16),
        grid_spec=pltpu.PrefetchScalarGridSpec(
            num_scalar_prefetch=1,
            grid=(heads, rows // block),
            in_specs=[
                pl.BlockSpec((block, head_size), lambda h, i, m: (i, h)),
                pl.BlockSpec((seq_len, head_size), lambda h, i, m: (0, 0)),
                pl.BlockSpec((seq_len, head_size), lambda h, i, m: (0, 1)),
            ],
            out_specs=pl.BlockSpec((block, head_size), lambda h, i, m: (i, h)),
        ),
        compiler_params=pltpu.CompilerParams(
            dimension_semantics=("arbitrary", "arbitrary"),
            vmem_limit_bytes=48 * 1024 * 1024,
        ),
    )(meta, q_rows, kv_all, kv_all)


def shards(
    queries, kv_pairs, residual, norm_gain, o_weight, w_in, w_down, expert_ids, route_weights
):
    tok_dev = queries.shape[0]
    width = residual.shape[1]
    n_sa = lax.axis_size("sa")
    n_sb = lax.axis_size("sb")
    n_seq = n_sa * n_sb
    n_grp = lax.axis_size("grp")
    devices = n_seq * n_grp
    head_size = HD
    heads_all = queries.shape[1] // head_size
    key_heads = kv_pairs.shape[2] // head_size
    sharing = heads_all // key_heads
    heads_here = heads_all // n_sa
    block_rows = o_weight.shape[0]
    assert sharing % heads_here == 0
    sa = lax.axis_index("sa")
    sb = lax.axis_index("sb")

    pair = lax.axis_index("grp") % 2
    half = o_weight.shape[1] // 2
    w_mine = lax.all_gather(
        lax.dynamic_slice_in_dim(o_weight, pair * half, half, axis=1), "sb", axis=0, tiled=True
    )
    q_send = queries.reshape(tok_dev, n_sa, heads_here * head_size).transpose(1, 0, 2)
    kv_heads = kv_pairs.reshape(2, tok_dev, key_heads, head_size)
    head_of_dest = (jnp.arange(n_sa) * heads_here) // sharing
    kv_send = jnp.take(kv_heads, head_of_dest, axis=2)
    kv_send = kv_send.transpose(2, 1, 0, 3).reshape(n_sa, tok_dev, 2 * head_size)
    packed = lax.all_to_all(
        jnp.concatenate([q_send, kv_send], axis=2), "sa", split_axis=0, concat_axis=0, tiled=True
    )
    q_rows = packed[:, :, : heads_here * head_size].reshape(n_sa * tok_dev, heads_here * head_size)
    kv_col = packed[:, :, heads_here * head_size :]
    kv_grid = lax.all_to_all(
        jnp.broadcast_to(kv_col[None], (n_sb,) + kv_col.shape), "sb", split_axis=0,
        concat_axis=0, tiled=True,
    )
    kv_all = kv_grid.transpose(1, 0, 2, 3).reshape(n_seq * tok_dev, 2 * head_size)
    meta = jnp.stack([sb, jnp.zeros_like(sb)]).astype(jnp.int32)
    attended = attention(meta, q_rows, kv_all, heads_here, head_size, tok_dev, n_sb)

    w_mine, attended = lax.optimization_barrier((w_mine, attended))
    w_other = lax.ppermute(w_mine, "grp", [(g, g ^ 1) for g in range(n_grp)])
    w_rows = jnp.concatenate([w_mine, w_other], axis=1)

    partial_sum = None
    for j in range(w_rows.shape[0] // block_rows):
        cols = slice(j * block_rows, (j + 1) * block_rows)
        partial_j = jnp.dot(
            attended[:, cols], w_rows[cols], preferred_element_type=jnp.float32
        ).astype(jnp.bfloat16).astype(jnp.float32)
        partial_sum = partial_j if partial_sum is None else partial_sum + partial_j
    swapped = lax.psum_scatter(
        partial_sum.astype(jnp.bfloat16), "sa", scatter_dimension=0, tiled=True
    )
    attn_out = lax.dynamic_slice_in_dim(
        jnp.concatenate([swapped, swapped], axis=1), pair * half, 2 * half, axis=1
    ).astype(jnp.float32)
    mixed = residual.astype(jnp.float32) + attn_out
    mean_square = jnp.mean(mixed * mixed, axis=1, keepdims=True)
    normed = (mixed * lax.rsqrt(mean_square + 1e-06) * norm_gain.astype(jnp.float32)).astype(
        jnp.bfloat16
    )

    top_count = expert_ids.shape[1]
    capacity = 2 * tok_dev * top_count // devices
    slots = devices * capacity
    flat_ids = expert_ids.reshape(-1)
    flat_weights = route_weights.reshape(-1)
    n_flat = flat_ids.shape[0]
    onehot = (flat_ids[:, None] == jnp.arange(devices, dtype=jnp.int32)[None, :]).astype(
        jnp.bfloat16
    )
    row = lax.broadcasted_iota(jnp.int32, (n_flat, n_flat), 0)
    col = lax.broadcasted_iota(jnp.int32, (n_flat, n_flat), 1)
    before = (col < row).astype(jnp.bfloat16)
    earlier = jnp.dot(before, onehot, preferred_element_type=jnp.float32)
    rank = jnp.sum(earlier * onehot.astype(jnp.float32), axis=1).astype(jnp.int32)
    slot_index = flat_ids * capacity + rank
    picks = slot_index[:, None] == jnp.arange(slots, dtype=jnp.int32)[None, :]
    token_slots = jnp.any(picks.reshape(tok_dev, top_count, slots), axis=1).astype(jnp.bfloat16)
    outgoing_rows = lax.dot_general(
        token_slots, normed, (((0,), (0,)), ((), ())), preferred_element_type=jnp.float32
    ).astype(jnp.bfloat16)
    outgoing_rows = outgoing_rows.reshape(devices, capacity, width)
    ffe_width = w_down.shape[1]
    arrived = lax.all_to_all(outgoing_rows, ("grp", "sa", "sb"), split_axis=0, concat_axis=0, tiled=True)
    flat_rows = arrived.reshape(-1, width)
    projected = jnp.dot(flat_rows, w_in[0], preferred_element_type=jnp.float32)
    hidden = (jax.nn.silu(projected[:, :ffe_width]) * projected[:, ffe_width:]).astype(jnp.bfloat16)
    produced = jnp.dot(hidden, w_down[0], preferred_element_type=jnp.float32).astype(jnp.bfloat16)
    returned = lax.all_to_all(
        produced.reshape(arrived.shape), ("grp", "sa", "sb"), split_axis=0, concat_axis=0, tiled=True
    )
    returned = returned.reshape(slots, width)
    placed = jnp.sum(
        jnp.where(picks, flat_weights[:, None], jnp.float32(0.0)).reshape(tok_dev, top_count, slots),
        axis=1,
    )
    high = placed.astype(jnp.bfloat16)
    rest = placed - high.astype(jnp.float32)
    middle = rest.astype(jnp.bfloat16)
    low = (rest - middle.astype(jnp.float32)).astype(jnp.bfloat16)
    parts = jnp.concatenate([high, middle, low], axis=0)
    combined = jnp.sum(
        jnp.dot(parts, returned, preferred_element_type=jnp.float32).reshape(3, tok_dev, width),
        axis=0,
    )
    return (mixed + combined).astype(jnp.bfloat16)


def solution(mesh):
    n_grp, n_seq = mesh.shape["grp"], mesh.shape["seq"]
    n_sb = math.isqrt(n_seq)
    grid = Mesh(mesh.devices.reshape(n_grp, n_seq // n_sb, n_sb), ("grp", "sa", "sb"))
    tokens = ("grp", "sa", "sb")
    return jax.shard_map(
        shards,
        mesh=grid,
        in_specs=(
            P(tokens, None),
            P(None, tokens, None),
            P(tokens, None),
            P(),
            P(("sa", "sb"), None),
            P(tokens, None, None),
            P(tokens, None, None),
            P(tokens, None),
            P(tokens, None),
        ),
        out_specs=P(tokens, None),
        check_vma=False,
    )
```
